512 devices in a mesh: frame: 8 (over y), space: 32 (over z, x), dp: 2 (over core).
Axes of the slice: x: 4, y: 8, z: 8, core: 2. Of those that a mesh axis runs over, the one named last changes fastest.
Arguments:
- frames_in: bfloat16 [16, 4096, 768], P(('dp', 'frame'), 'space'), parts along dimension 0, may hold values from -6 to 6
- cotangent: bfloat16 [16, 4096, 768], P(('dp', 'frame'), 'space'), parts along dimension 0, may hold values from -6 to 6
- w_qkv_space: bfloat16 [768, 2304], P('space'), may hold values from -0.21875 to 0.21875
- w_out_space: bfloat16 [768, 768], P('space'), may hold values from -0.875 to 0.875
- w_qkv_time: bfloat16 [768, 2304], P('space'), may hold values from -0.21875 to 0.21875
- w_out_time: bfloat16 [768, 768], P('space'), may hold values from -0.21875 to 0.21875
- neighbours: int32 [32, 4], replicated, may hold values from 0 to 31, as said below
Outputs:
- frames_out: bfloat16 [16, 4096, 768], P(('dp', 'frame'), 'space'), parts along dimension 0
- grad_frames: bfloat16 [16, 4096, 768], P(('dp', 'frame'), 'space'), parts along dimension 0
The draws below stay inside these ranges and needn't reach their ends.
There are 2 independent parts, one for each index of `dp`. The reference program is written for one: setup_inputs(seed, part) draws one part's arguments, and reference() takes and returns one part's arrays. A program takes and returns all parts, laid end to end along the dimension named above; an argument that names none is the same for every part. Nothing has to cross between parts.
Inputs may be any that keep to these rules, and one draw needn't show every extreme that they name: `neighbours`: row b lists block b first; every entry c satisfies |c - b| <= 1; entries may repeat, and a repeated entry counts once.
All inputs are finite; a program needn't handle non-finite values.
Results may differ from the reference program's by a relative error of at most 0.023.
Values may be sent and summed in bfloat16 or wider, within the bound.
No kernel may reach another device: no remote copies, remote signals or barrier semaphores. Data moves between devices by JAX's collectives and lax.ppermute only.
A program may use at most 64 MiB of HBM per device.

```python
import jax
import jax.numpy as jnp
from jax import lax

D = 768
HEADS = 12
HD = 64
BLOCK = 128
KNB = 4
BLK_DEV = 1
NBLK = 32
FTOK = 4096
FRAMES = 8
N_SPACE = 32


def draw_neighbours(key, part):
    block_ids = jnp.arange(NBLK, dtype=jnp.int32)
    offsets = jax.random.randint(key, (NBLK, KNB - 1), -BLK_DEV, BLK_DEV + 1, dtype=jnp.int32)
    others = jnp.clip(block_ids[:, None] + offsets, 0, NBLK - 1)
    return jnp.concatenate([block_ids[:, None], others], axis=1).astype(jnp.int32)


def block_levels(rng, dims, cuts, smallest, largest):
    def one(dim, shards_of):
        draws = jax.random.uniform(jax.random.fold_in(jax.random.fold_in(rng, 6), dim), (shards_of,), jnp.float32, smallest / len(cuts), largest / len(cuts))
        return jnp.repeat(jnp.exp(draws), dims[dim] // shards_of).reshape((-1,) + (1,) * (len(dims) - dim - 1))

    loudness = one(*cuts[0])
    for cut in cuts[1:]:
        loudness = loudness * one(*cut)
    return loudness


def normal_values(own_key, extent, deviation, reach, cuts=(), held_as=jnp.bfloat16):
    drawn = deviation * jax.random.normal(own_key, extent, jnp.float32)
    if cuts:
        drawn = drawn * block_levels(own_key, extent, cuts, -0.22, 0.18)
    return jnp.clip(drawn, -reach, reach).astype(held_as)


def setup_inputs(seed: int = 0, part: int = 0) -> dict:
    seeds = jax.random.split(jax.random.key(seed), 8)
    part_splits = jax.random.split(jax.random.fold_in(seeds[7], part), 8)
    frames_in = normal_values(part_splits[0], (FRAMES, FTOK, D), 1.0, 6.0, ((0, 8), (1, 32)))
    cotangent = normal_values(part_splits[1], (FRAMES, FTOK, D), 1.0, 6.0, ((0, 8), (1, 32)))
    w_qkv_space = normal_values(seeds[2], (D, 3 * D), D ** -0.5, 0.21875, ((0, 32),))
    w_out_space = normal_values(seeds[3], (D, D), (D // 16) ** -0.5, 0.875, ((0, 32),))
    w_qkv_time = normal_values(seeds[4], (D, 3 * D), D ** -0.5, 0.21875, ((0, 32),))
    w_out_time = normal_values(seeds[5], (D, D), D ** -0.5, 0.21875, ((0, 32),))
    neighbours = draw_neighbours(jax.random.fold_in(seeds[7], 71), part)
    return dict(frames_in=frames_in, cotangent=cotangent, w_qkv_space=w_qkv_space, w_out_space=w_out_space, w_qkv_time=w_qkv_time, w_out_time=w_out_time, neighbours=neighbours)


EPS = 1e-06

def widen(array):
    return lax.optimization_barrier(array).astype(jnp.float32)

def rms_norm(row_data):
    values = row_data.astype(jnp.float32)
    factor = lax.rsqrt(lax.optimization_barrier(jnp.mean(values * values, axis=-1, keepdims=True)) + EPS)
    return (values * factor).astype(jnp.bfloat16)

def rms_back(row_data, upstream):
    values = row_data.astype(jnp.float32)
    factor = lax.rsqrt(lax.optimization_barrier(jnp.mean(values * values, axis=-1, keepdims=True)) + EPS)
    inner_mean = lax.optimization_barrier(jnp.mean(values * upstream, axis=-1, keepdims=True))
    return factor * upstream - values * factor ** 3 * inner_mean

def block_mask(neighbour_rows, first_id):
    block_count = neighbour_rows.shape[0]
    candidate = first_id + jnp.arange(3 * block_count, dtype=jnp.int32)
    matches = jnp.any(neighbour_rows[:, :, None] == candidate[None, None, :], axis=1)
    return jnp.repeat(jnp.repeat(matches, BLOCK, axis=0), BLOCK, axis=1)

def space_attend(queries, key_rows, value_rows, allowed):
    score_scale = HD ** (-0.5)
    query_count = queries.shape[0]
    key_count = key_rows.shape[0]
    output_list = []
    total_list = []
    for head_pair in range(HEADS // 2):
        start_col = head_pair * 2 * HD
        stop_col = start_col + 2 * HD
        query_part = widen(queries[:, start_col:stop_col].reshape(query_count, 2, HD))
        key_part = widen(key_rows[:, start_col:stop_col].reshape(key_count, 2, HD))
        value_part = widen(value_rows[:, start_col:stop_col].reshape(key_count, 2, HD))
        scores = jnp.einsum('sgh,tgh->gst', query_part, key_part) * score_scale
        exponent = jnp.where(allowed[None], jnp.exp(scores), 0.0)
        totals = lax.optimization_barrier(jnp.sum(exponent, axis=-1))
        probability = (exponent / totals[:, :, None]).astype(jnp.bfloat16)
        combined = jnp.einsum('gst,tgh->sgh', widen(probability), value_part)
        output_list.append(combined.astype(jnp.bfloat16).reshape(query_count, 2 * HD))
        total_list.append(totals)
    return (jnp.concatenate(output_list, axis=1), jnp.concatenate(total_list, axis=0))

def space_back(queries, key_rows, value_rows, allowed, totals, attended, grad_attended):
    score_scale = HD ** (-0.5)
    query_count = queries.shape[0]
    key_count = key_rows.shape[0]
    query_list = []
    key_list = []
    value_list = []
    for head_pair in range(HEADS // 2):
        start_col = head_pair * 2 * HD
        stop_col = start_col + 2 * HD
        query_part = widen(queries[:, start_col:stop_col].reshape(query_count, 2, HD))
        key_part = widen(key_rows[:, start_col:stop_col].reshape(key_count, 2, HD))
        value_part = widen(value_rows[:, start_col:stop_col].reshape(key_count, 2, HD))
        out_part = widen(attended[:, start_col:stop_col].reshape(query_count, 2, HD))
        grad_part = widen(grad_attended[:, start_col:stop_col].reshape(query_count, 2, HD))
        scores = jnp.einsum('sgh,tgh->gst', query_part, key_part) * score_scale
        exponent = jnp.where(allowed[None], jnp.exp(scores), 0.0)
        weight = exponent / totals[2 * head_pair:2 * head_pair + 2, :, None]
        probability = weight.astype(jnp.bfloat16)
        prob_grad = jnp.einsum('sgh,tgh->gst', grad_part, value_part)
        row_delta = jnp.einsum('sgh,sgh->gs', grad_part, out_part)
        score_grad = (weight * (prob_grad - row_delta[:, :, None])).astype(jnp.bfloat16)
        query_grad = jnp.einsum('gst,tgh->sgh', widen(score_grad), key_part) * score_scale
        key_grad = jnp.einsum('gst,sgh->tgh', widen(score_grad), query_part) * score_scale
        value_grad = jnp.einsum('gst,sgh->tgh', widen(probability), grad_part)
        query_list.append(query_grad.astype(jnp.bfloat16).reshape(query_count, 2 * HD))
        key_list.append(key_grad.reshape(key_count, 2 * HD))
        value_list.append(value_grad.reshape(key_count, 2 * HD))
    return (jnp.concatenate(query_list, axis=1), jnp.concatenate(key_list, axis=1), jnp.concatenate(value_list, axis=1))

def time_attend(queries, key_rows, value_rows):
    frame_count, position_count, feature_count = queries.shape
    split_shape = (frame_count, position_count, HEADS, HD)
    score_scale = HD ** (-0.5)
    scores = jnp.einsum('fphd,gphd->phfg', widen(queries.reshape(split_shape)), widen(key_rows.reshape(split_shape))) * score_scale
    causal = jnp.arange(frame_count)[:, None] >= jnp.arange(frame_count)[None, :]
    exponent = jnp.where(causal, jnp.exp(scores), 0.0)
    totals = lax.optimization_barrier(jnp.sum(exponent, axis=-1))
    probability = (exponent / totals[..., None]).astype(jnp.bfloat16)
    combined = jnp.einsum('phfg,gphd->fphd', widen(probability), widen(value_rows.reshape(split_shape)))
    return (combined.astype(jnp.bfloat16).reshape(frame_count, position_count, feature_count), totals)

def time_back(queries, key_rows, value_rows, attended, grad_attended, totals):
    frame_count, position_count, feature_count = queries.shape
    split_shape = (frame_count, position_count, HEADS, HD)
    score_scale = HD ** (-0.5)
    query_four = widen(queries.reshape(split_shape))
    key_four = widen(key_rows.reshape(split_shape))
    value_four = widen(value_rows.reshape(split_shape))
    out_four = widen(attended.reshape(split_shape))
    grad_four = widen(grad_attended.reshape(split_shape))
    scores = jnp.einsum('fphd,gphd->phfg', query_four, key_four) * score_scale
    causal = jnp.arange(frame_count)[:, None] >= jnp.arange(frame_count)[None, :]
    exponent = jnp.where(causal, jnp.exp(scores), 0.0)
    weight = exponent / totals[..., None]
    probability = weight.astype(jnp.bfloat16)
    prob_grad = jnp.einsum('fphd,gphd->phfg', grad_four, value_four)
    row_delta = jnp.einsum('fphd,fphd->phf', grad_four, out_four)
    score_grad = (weight * (prob_grad - row_delta[..., None])).astype(jnp.bfloat16)
    query_grad = jnp.einsum('phfg,gphd->fphd', widen(score_grad), key_four) * score_scale
    key_grad = jnp.einsum('phfg,fphd->gphd', widen(score_grad), query_four) * score_scale
    value_grad = jnp.einsum('phfg,fphd->gphd', widen(probability), grad_four)
    pieces = [gradient.astype(jnp.bfloat16).reshape(frame_count, position_count, feature_count) for gradient in (query_grad, key_grad, value_grad)]
    return jnp.concatenate(pieces, axis=-1)

def time_block(stream_rows, grad_rows, qkv_weight, out_weight):
    frame_count, position_count, feature_count = stream_rows.shape
    flat_count = frame_count * position_count
    normed = rms_norm(stream_rows).reshape(flat_count, feature_count)
    projected = jnp.dot(normed, qkv_weight, preferred_element_type=jnp.float32).astype(jnp.bfloat16)
    projected = projected.reshape(frame_count, position_count, 3 * feature_count)
    queries = projected[..., :feature_count]
    key_rows = projected[..., feature_count:2 * feature_count]
    value_rows = projected[..., 2 * feature_count:]
    attended, totals = time_attend(queries, key_rows, value_rows)
    update = jnp.dot(attended.reshape(flat_count, feature_count), out_weight, preferred_element_type=jnp.float32)
    out_rows = (stream_rows.astype(jnp.float32) + update.reshape(stream_rows.shape)).astype(jnp.bfloat16)
    grad_attended = jnp.dot(grad_rows.reshape(flat_count, feature_count), out_weight.T, preferred_element_type=jnp.float32).astype(jnp.bfloat16).reshape(stream_rows.shape)
    gradients = time_back(queries, key_rows, value_rows, attended, grad_attended, totals)
    grad_normed = jnp.dot(gradients.reshape(flat_count, 3 * feature_count), qkv_weight.T, preferred_element_type=jnp.float32).reshape(stream_rows.shape)
    grad_stream = (grad_rows.astype(jnp.float32) + rms_back(stream_rows, grad_normed)).astype(jnp.bfloat16)
    return (out_rows, grad_stream)

def windows(shards):
    zero_shard = jnp.zeros((1,) + shards.shape[1:], shards.dtype)
    padded = jnp.concatenate([zero_shard, shards, zero_shard], axis=0)
    return jnp.concatenate([padded[:-2], padded[1:-1], padded[2:]], axis=1)

def combine(partial_value, shard):
    own_part = partial_value[:, shard:2 * shard]
    lower_part = lax.optimization_barrier(partial_value[:, :shard].astype(jnp.bfloat16))
    upper_part = lax.optimization_barrier(partial_value[:, 2 * shard:].astype(jnp.bfloat16))
    zero_shard = jnp.zeros((1,) + lower_part.shape[1:], jnp.bfloat16)
    from_prev = jnp.concatenate([zero_shard, upper_part[:-1]], axis=0)
    from_next = jnp.concatenate([lower_part[1:], zero_shard], axis=0)
    summed = own_part + from_prev.astype(jnp.float32) + from_next.astype(jnp.float32)
    return summed.astype(jnp.bfloat16)

def reference(frames_in, cotangent, w_qkv_space, w_out_space, w_qkv_time, w_out_time, neighbours):
    frame_count, frame_tokens, feature_count = frames_in.shape
    shard = BLK_DEV * BLOCK
    device_lists = neighbours.reshape(N_SPACE, BLK_DEV, KNB)
    device_ids = jnp.arange(N_SPACE, dtype=jnp.int32)

    def space_setup(frame_in):
        normed = rms_norm(frame_in)
        projected = jnp.dot(normed, w_qkv_space, preferred_element_type=jnp.float32).astype(jnp.bfloat16)
        queries = projected[:, :feature_count].reshape(N_SPACE, shard, feature_count)
        key_window = windows(projected[:, feature_count:2 * feature_count].reshape(N_SPACE, shard, feature_count))
        value_window = windows(projected[:, 2 * feature_count:].reshape(N_SPACE, shard, feature_count))

        def one_device(item):
            query_rows, key_rows, value_rows, lists_here, device_id = item
            allowed = block_mask(lists_here, (device_id - 1) * BLK_DEV)
            return space_attend(query_rows, key_rows, value_rows, allowed)
        attended, totals = lax.map(one_device, (queries, key_window, value_window, device_lists, device_ids))
        return (queries, key_window, value_window, attended, totals)

    def space_forward(frame_in):
        attended = space_setup(frame_in)[3]
        update = jnp.dot(attended.reshape(frame_tokens, feature_count), w_out_space, preferred_element_type=jnp.float32)
        return (frame_in.astype(jnp.float32) + update).astype(jnp.bfloat16)
    stream = lax.map(space_forward, frames_in)
    stream_dev = stream.reshape(frame_count, N_SPACE, shard, feature_count).transpose(1, 0, 2, 3)
    grad_dev = cotangent.reshape(frame_count, N_SPACE, shard, feature_count).transpose(1, 0, 2, 3)

    def time_device(item):
        return time_block(item[0], item[1], w_qkv_time, w_out_time)
    out_dev, stream_grad_dev = lax.map(time_device, (stream_dev, grad_dev))
    frames_out = out_dev.transpose(1, 0, 2, 3).reshape(frame_count, frame_tokens, feature_count)
    grad_stream = stream_grad_dev.transpose(1, 0, 2, 3).reshape(frame_count, frame_tokens, feature_count)

    def space_backward(item):
        frame_in, grad_frame = item
        queries, key_window, value_window, attended, totals = space_setup(frame_in)
        grad_attended = jnp.dot(grad_frame, w_out_space.T, preferred_element_type=jnp.float32)
        grad_attended = grad_attended.astype(jnp.bfloat16).reshape(N_SPACE, shard, feature_count)

        def one_device(parts):
            query_rows, key_rows, value_rows, lists_here, device_id, attended_rows, total_rows, grad_rows = parts
            allowed = block_mask(lists_here, (device_id - 1) * BLK_DEV)
            return space_back(query_rows, key_rows, value_rows, allowed, total_rows, attended_rows, grad_rows)
        grad_query, key_partial, value_partial = lax.map(one_device, (queries, key_window, value_window, device_lists, device_ids, attended, totals, grad_attended))
        grad_key = combine(key_partial, shard)
        grad_value = combine(value_partial, shard)
        grad_project = jnp.concatenate([grad_query, grad_key, grad_value], axis=-1)
        grad_normed = jnp.dot(grad_project.reshape(frame_tokens, 3 * feature_count), w_qkv_space.T, preferred_element_type=jnp.float32)
        return (grad_frame.astype(jnp.float32) + rms_back(frame_in, grad_normed)).astype(jnp.bfloat16)
    grad_frames = lax.map(space_backward, (frames_in, grad_stream))
    return (frames_out, grad_frames)
```

```python
import jax
import jax.numpy as jnp
from jax import lax
from jax.sharding import PartitionSpec as P

HEADS = 12
HD = 64
BLOCK = 128


EPS = 1e-06


def padded(cells, sides, width):
    for axis, dim in sides:
        count = lax.axis_size(axis)
        ends = count - 1
        head = lax.slice_in_dim(cells, 0, width, axis=dim)
        tail = lax.slice_in_dim(cells, cells.shape[dim] - width, cells.shape[dim], axis=dim)
        cells = jnp.concatenate(
            [
                lax.ppermute(tail, axis, [(i, (i + 1) % count) for i in range(ends)]),
                cells,
                lax.ppermute(head, axis, [((i + 1) % count, i) for i in range(ends)]),
            ],
            axis=dim,
        )
    return cells


def rms_norm(row_data):
    values = row_data.astype(jnp.float32)
    factor = lax.rsqrt(jnp.mean(values * values, axis=-1, keepdims=True) + EPS)
    return (values * factor).astype(jnp.bfloat16)


def rms_back(row_data, upstream):
    values = row_data.astype(jnp.float32)
    factor = lax.rsqrt(jnp.mean(values * values, axis=-1, keepdims=True) + EPS)
    inner_mean = jnp.mean(values * upstream, axis=-1, keepdims=True)
    return factor * upstream - values * factor**3 * inner_mean


def block_mask(neighbour_rows, first_id):
    block_count = neighbour_rows.shape[0]
    candidate = first_id + jnp.arange(3 * block_count, dtype=jnp.int32)
    matches = jnp.any(neighbour_rows[:, :, None] == candidate[None, None, :], axis=1)
    return jnp.repeat(jnp.repeat(matches, BLOCK, axis=0), BLOCK, axis=1)


def space_attend(queries, key_rows, value_rows, allowed):
    score_scale = HD ** (-0.5)
    query_count = queries.shape[0]
    key_count = key_rows.shape[0]
    output_list = []
    total_list = []
    for head_pair in range(HEADS // 2):
        start_col = head_pair * 2 * HD
        stop_col = start_col + 2 * HD
        query_part = queries[:, start_col:stop_col].reshape(query_count, 2, HD)
        key_part = key_rows[:, start_col:stop_col].reshape(key_count, 2, HD)
        value_part = value_rows[:, start_col:stop_col].reshape(key_count, 2, HD)
        scores = (
            jnp.einsum("sgh,tgh->gst", query_part, key_part, preferred_element_type=jnp.float32)
            * score_scale
        )
        exponent = jnp.where(allowed[None], jnp.exp(scores), 0.0)
        totals = jnp.sum(exponent, axis=-1)
        probability = (exponent / totals[:, :, None]).astype(jnp.bfloat16)
        combined = jnp.einsum(
            "gst,tgh->sgh", probability, value_part, preferred_element_type=jnp.float32
        )
        output_list.append(combined.astype(jnp.bfloat16).reshape(query_count, 2 * HD))
        total_list.append(totals)
    return (jnp.concatenate(output_list, axis=1), jnp.concatenate(total_list, axis=0))


def space_back(queries, key_rows, value_rows, allowed, totals, attended, grad_attended):
    score_scale = HD ** (-0.5)
    query_count = queries.shape[0]
    key_count = key_rows.shape[0]
    query_list = []
    key_list = []
    value_list = []
    for head_pair in range(HEADS // 2):
        start_col = head_pair * 2 * HD
        stop_col = start_col + 2 * HD
        query_part = queries[:, start_col:stop_col].reshape(query_count, 2, HD)
        key_part = key_rows[:, start_col:stop_col].reshape(key_count, 2, HD)
        value_part = value_rows[:, start_col:stop_col].reshape(key_count, 2, HD)
        out_part = attended[:, start_col:stop_col].reshape(query_count, 2, HD)
        grad_part = grad_attended[:, start_col:stop_col].reshape(query_count, 2, HD)
        scores = (
            jnp.einsum("sgh,tgh->gst", query_part, key_part, preferred_element_type=jnp.float32)
            * score_scale
        )
        exponent = jnp.where(allowed[None], jnp.exp(scores), 0.0)
        weight = exponent / totals[2 * head_pair : 2 * head_pair + 2, :, None]
        probability = weight.astype(jnp.bfloat16)
        prob_grad = jnp.einsum(
            "sgh,tgh->gst", grad_part, value_part, preferred_element_type=jnp.float32
        )
        row_delta = jnp.einsum(
            "sgh,sgh->gs", grad_part, out_part, preferred_element_type=jnp.float32
        )
        score_grad = (weight * (prob_grad - row_delta[:, :, None])).astype(jnp.bfloat16)
        query_grad = (
            jnp.einsum("gst,tgh->sgh", score_grad, key_part, preferred_element_type=jnp.float32)
            * score_scale
        )
        key_grad = (
            jnp.einsum("gst,sgh->tgh", score_grad, query_part, preferred_element_type=jnp.float32)
            * score_scale
        )
        value_grad = jnp.einsum(
            "gst,sgh->tgh", probability, grad_part, preferred_element_type=jnp.float32
        )
        query_list.append(query_grad.astype(jnp.bfloat16).reshape(query_count, 2 * HD))
        key_list.append(key_grad.reshape(key_count, 2 * HD))
        value_list.append(value_grad.reshape(key_count, 2 * HD))
    return (
        jnp.concatenate(query_list, axis=1),
        jnp.concatenate(key_list, axis=1),
        jnp.concatenate(value_list, axis=1),
    )


def time_attend(queries, key_rows, value_rows):
    frame_count, position_count, feature_count = queries.shape
    split_shape = (frame_count, position_count, HEADS, HD)
    score_scale = HD ** (-0.5)
    scores = (
        jnp.einsum(
            "fphd,gphd->phfg",
            queries.reshape(split_shape),
            key_rows.reshape(split_shape),
            preferred_element_type=jnp.float32,
        )
        * score_scale
    )
    causal = jnp.arange(frame_count)[:, None] >= jnp.arange(frame_count)[None, :]
    exponent = jnp.where(causal, jnp.exp(scores), 0.0)
    totals = jnp.sum(exponent, axis=-1)
    probability = (exponent / totals[..., None]).astype(jnp.bfloat16)
    combined = jnp.einsum(
        "phfg,gphd->fphd",
        probability,
        value_rows.reshape(split_shape),
        preferred_element_type=jnp.float32,
    )
    return (
        combined.astype(jnp.bfloat16).reshape(frame_count, position_count, feature_count),
        totals,
    )


def time_back(queries, key_rows, value_rows, attended, grad_attended, totals):
    frame_count, position_count, feature_count = queries.shape
    split_shape = (frame_count, position_count, HEADS, HD)
    score_scale = HD ** (-0.5)
    query_four = queries.reshape(split_shape)
    key_four = key_rows.reshape(split_shape)
    value_four = value_rows.reshape(split_shape)
    out_four = attended.reshape(split_shape)
    grad_four = grad_attended.reshape(split_shape)
    scores = (
        jnp.einsum("fphd,gphd->phfg", query_four, key_four, preferred_element_type=jnp.float32)
        * score_scale
    )
    causal = jnp.arange(frame_count)[:, None] >= jnp.arange(frame_count)[None, :]
    exponent = jnp.where(causal, jnp.exp(scores), 0.0)
    weight = exponent / totals[..., None]
    probability = weight.astype(jnp.bfloat16)
    prob_grad = jnp.einsum(
        "fphd,gphd->phfg", grad_four, value_four, preferred_element_type=jnp.float32
    )
    row_delta = jnp.einsum(
        "fphd,fphd->phf", grad_four, out_four, preferred_element_type=jnp.float32
    )
    score_grad = (weight * (prob_grad - row_delta[..., None])).astype(jnp.bfloat16)
    query_grad = (
        jnp.einsum("phfg,gphd->fphd", score_grad, key_four, preferred_element_type=jnp.float32)
        * score_scale
    )
    key_grad = (
        jnp.einsum("phfg,fphd->gphd", score_grad, query_four, preferred_element_type=jnp.float32)
        * score_scale
    )
    value_grad = jnp.einsum(
        "phfg,fphd->gphd", probability, grad_four, preferred_element_type=jnp.float32
    )
    pieces = [
        gradient.astype(jnp.bfloat16).reshape(frame_count, position_count, feature_count)
        for gradient in (query_grad, key_grad, value_grad)
    ]
    return jnp.concatenate(pieces, axis=-1)


def to_frames(local_rows):
    return lax.all_to_all(local_rows[None], "frame", split_axis=1, concat_axis=0, tiled=True)


def to_space(frame_rows):
    return lax.all_to_all(frame_rows, "frame", split_axis=0, concat_axis=1, tiled=True)[0]


def rim(first_part, second_part, width):
    return (padded(first_part, (("space", 0),), width), padded(second_part, (("space", 0),), width))


def local(frames_in, cotangent, w_qkv_space, w_out_space, w_qkv_time, w_out_time, neighbours):
    local_in = frames_in[0]
    grad_out = cotangent[0]
    shard, feature_count = local_in.shape
    weight_rows = jnp.concatenate([w_qkv_space, w_out_space, w_qkv_time, w_out_time], axis=1)
    all_weights = lax.all_gather(weight_rows, "space", axis=0, tiled=True)
    widths = [w_qkv_space.shape[1], w_out_space.shape[1], w_qkv_time.shape[1], w_out_time.shape[1]]
    bounds = [0]
    for width in widths:
        bounds.append(bounds[-1] + width)
    full_qkv_space, full_out_space, full_qkv_time, full_out_time = (
        all_weights[:, bounds[index] : bounds[index + 1]] for index in range(4)
    )
    block_count = shard // BLOCK
    space_index = lax.axis_index("space")
    lists_here = lax.dynamic_slice_in_dim(neighbours, space_index * block_count, block_count, 0)
    allowed = block_mask(lists_here, (space_index - 1) * block_count)
    normed_space = rms_norm(local_in)
    projected = jnp.dot(normed_space, full_qkv_space, preferred_element_type=jnp.float32).astype(
        jnp.bfloat16
    )
    queries = projected[:, :feature_count]
    key_window, value_window = rim(
        projected[:, feature_count : 2 * feature_count], projected[:, 2 * feature_count :], shard
    )
    attended, totals = space_attend(queries, key_window, value_window, allowed)
    update = jnp.dot(attended, full_out_space, preferred_element_type=jnp.float32)
    stream = (local_in.astype(jnp.float32) + update).astype(jnp.bfloat16)
    normed_time = rms_norm(stream)
    projected_time = jnp.dot(normed_time, full_qkv_time, preferred_element_type=jnp.float32).astype(
        jnp.bfloat16
    )
    time_rows = to_frames(projected_time)
    query_time = time_rows[..., :feature_count]
    key_time = time_rows[..., feature_count : 2 * feature_count]
    value_time = time_rows[..., 2 * feature_count :]
    attended_time, totals_time = time_attend(query_time, key_time, value_time)
    attended_back = to_space(attended_time)
    update_time = jnp.dot(attended_back, full_out_time, preferred_element_type=jnp.float32)
    frames_out = (stream.astype(jnp.float32) + update_time).astype(jnp.bfloat16)
    grad_att_time = jnp.dot(grad_out, full_out_time.T, preferred_element_type=jnp.float32).astype(
        jnp.bfloat16
    )
    grad_time_rows = to_frames(grad_att_time)
    gradients = time_back(
        query_time, key_time, value_time, attended_time, grad_time_rows, totals_time
    )
    grad_project_time = to_space(gradients)
    grad_normed_time = jnp.dot(
        grad_project_time, full_qkv_time.T, preferred_element_type=jnp.float32
    )
    grad_stream = (grad_out.astype(jnp.float32) + rms_back(stream, grad_normed_time)).astype(
        jnp.bfloat16
    )
    grad_attended = jnp.dot(
        grad_stream, full_out_space.T, preferred_element_type=jnp.float32
    ).astype(jnp.bfloat16)
    grad_query, key_partial, value_partial = space_back(
        queries, key_window, value_window, allowed, totals, attended, grad_attended
    )
    key_send = jnp.concatenate([key_partial[:shard], key_partial[2 * shard :]], axis=0).astype(
        jnp.bfloat16
    )
    value_send = jnp.concatenate(
        [value_partial[:shard], value_partial[2 * shard :]], axis=0
    ).astype(jnp.bfloat16)
    key_got, value_got = rim(key_send, value_send, shard)
    grad_key = (
        key_partial[shard : 2 * shard]
        + key_got[:shard].astype(jnp.float32)
        + key_got[3 * shard :].astype(jnp.float32)
    ).astype(jnp.bfloat16)
    grad_value = (
        value_partial[shard : 2 * shard]
        + value_got[:shard].astype(jnp.float32)
        + value_got[3 * shard :].astype(jnp.float32)
    ).astype(jnp.bfloat16)
    grad_project = jnp.concatenate([grad_query, grad_key, grad_value], axis=1)
    grad_normed = jnp.dot(grad_project, full_qkv_space.T, preferred_element_type=jnp.float32)
    grad_in = (grad_stream.astype(jnp.float32) + rms_back(local_in, grad_normed)).astype(
        jnp.bfloat16
    )
    return (frames_out[None], grad_in[None])


def solution(mesh):
    in_specs = (
        P(("dp", "frame"), "space", None),
        P(("dp", "frame"), "space", None),
        P("space", None),
        P("space", None),
        P("space", None),
        P("space", None),
        P(),
    )
    out_specs = (P(("dp", "frame"), "space", None), P(("dp", "frame"), "space", None))
    return jax.shard_map(local, mesh=mesh, in_specs=in_specs, out_specs=out_specs, check_vma=False)
```

```python
import jax
import jax.numpy as jnp
from jax import lax
from jax.sharding import PartitionSpec as P

HEADS = 12
HD = 64
BLOCK = 128


EPS = 1e-06


def padded(cells, sides, width):
    for axis, dim in sides:
        count = lax.axis_size(axis)
        ends = count - 1
        head = lax.slice_in_dim(cells, 0, width, axis=dim)
        tail = lax.slice_in_dim(cells, cells.shape[dim] - width, cells.shape[dim], axis=dim)
        cells = jnp.concatenate(
            [
                lax.ppermute(tail, axis, [(i, (i + 1) % count) for i in range(ends)]),
                cells,
                lax.ppermute(head, axis, [((i + 1) % count, i) for i in range(ends)]),
            ],
            axis=dim,
        )
    return cells


def rms_norm(row_data):
    values = row_data.astype(jnp.float32)
    factor = lax.rsqrt(jnp.mean(values * values, axis=-1, keepdims=True) + EPS)
    return (values * factor).astype(jnp.bfloat16)


def rms_back(row_data, upstream):
    values = row_data.astype(jnp.float32)
    factor = lax.rsqrt(jnp.mean(values * values, axis=-1, keepdims=True) + EPS)
    inner_mean = jnp.mean(values * upstream, axis=-1, keepdims=True)
    return factor * upstream - values * factor**3 * inner_mean


def block_mask(neighbour_rows, first_id):
    block_count = neighbour_rows.shape[0]
    candidate = first_id + jnp.arange(3 * block_count, dtype=jnp.int32)
    matches = jnp.any(neighbour_rows[:, :, None] == candidate[None, None, :], axis=1)
    return jnp.repeat(jnp.repeat(matches, BLOCK, axis=0), BLOCK, axis=1)


def space_attend(queries, key_rows, value_rows, allowed):
    score_scale = HD ** (-0.5)
    query_count = queries.shape[0]
    key_count = key_rows.shape[0]
    query_heads = queries.reshape(query_count, HEADS, HD)
    key_heads = key_rows.reshape(key_count, HEADS, HD)
    value_heads = value_rows.reshape(key_count, HEADS, HD)
    scores = (
        jnp.einsum("sgh,tgh->gst", query_heads, key_heads, preferred_element_type=jnp.float32)
        * score_scale
    )
    exponent = jnp.where(allowed[None], jnp.exp(scores), 0.0)
    totals = jnp.sum(exponent, axis=-1)
    probability = (exponent / totals[:, :, None]).astype(jnp.bfloat16)
    combined = jnp.einsum(
        "gst,tgh->sgh", probability, value_heads, preferred_element_type=jnp.float32
    )
    return combined.astype(jnp.bfloat16).reshape(query_count, HEADS * HD), totals


def space_back(queries, key_rows, value_rows, allowed, totals, attended, grad_attended):
    score_scale = HD ** (-0.5)
    query_count = queries.shape[0]
    key_count = key_rows.shape[0]
    query_heads = queries.reshape(query_count, HEADS, HD)
    key_heads = key_rows.reshape(key_count, HEADS, HD)
    value_heads = value_rows.reshape(key_count, HEADS, HD)
    out_heads = attended.reshape(query_count, HEADS, HD)
    grad_heads = grad_attended.reshape(query_count, HEADS, HD)
    scores = (
        jnp.einsum("sgh,tgh->gst", query_heads, key_heads, preferred_element_type=jnp.float32)
        * score_scale
    )
    exponent = jnp.where(allowed[None], jnp.exp(scores), 0.0)
    weight = exponent / totals[:, :, None]
    probability = weight.astype(jnp.bfloat16)
    prob_grad = jnp.einsum(
        "sgh,tgh->gst", grad_heads, value_heads, preferred_element_type=jnp.float32
    )
    row_delta = jnp.einsum(
        "sgh,sgh->gs", grad_heads, out_heads, preferred_element_type=jnp.float32
    )
    score_grad = (weight * (prob_grad - row_delta[:, :, None])).astype(jnp.bfloat16)
    query_grad = (
        jnp.einsum("gst,tgh->sgh", score_grad, key_heads, preferred_element_type=jnp.float32)
        * score_scale
    )
    key_grad = (
        jnp.einsum("gst,sgh->tgh", score_grad, query_heads, preferred_element_type=jnp.float32)
        * score_scale
    )
    value_grad = jnp.einsum(
        "gst,sgh->tgh", probability, grad_heads, preferred_element_type=jnp.float32
    )
    return (
        query_grad.astype(jnp.bfloat16).reshape(query_count, HEADS * HD),
        key_grad.reshape(key_count, HEADS * HD),
        value_grad.reshape(key_count, HEADS * HD),
    )


def time_attend(queries, key_rows, value_rows):
    frame_count, position_count, feature_count = queries.shape
    split_shape = (frame_count, position_count, HEADS, HD)
    score_scale = HD ** (-0.5)
    scores = (
        jnp.einsum(
            "fphd,gphd->phfg",
            queries.reshape(split_shape),
            key_rows.reshape(split_shape),
            preferred_element_type=jnp.float32,
        )
        * score_scale
    )
    causal = jnp.arange(frame_count)[:, None] >= jnp.arange(frame_count)[None, :]
    exponent = jnp.where(causal, jnp.exp(scores), 0.0)
    totals = jnp.sum(exponent, axis=-1)
    probability = (exponent / totals[..., None]).astype(jnp.bfloat16)
    combined = jnp.einsum(
        "phfg,gphd->fphd",
        probability,
        value_rows.reshape(split_shape),
        preferred_element_type=jnp.float32,
    )
    return (
        combined.astype(jnp.bfloat16).reshape(frame_count, position_count, feature_count),
        totals,
    )


def time_back(queries, key_rows, value_rows, attended, grad_attended, totals):
    frame_count, position_count, feature_count = queries.shape
    split_shape = (frame_count, position_count, HEADS, HD)
    score_scale = HD ** (-0.5)
    query_four = queries.reshape(split_shape)
    key_four = key_rows.reshape(split_shape)
    value_four = value_rows.reshape(split_shape)
    out_four = attended.reshape(split_shape)
    grad_four = grad_attended.reshape(split_shape)
    scores = (
        jnp.einsum("fphd,gphd->phfg", query_four, key_four, preferred_element_type=jnp.float32)
        * score_scale
    )
    causal = jnp.arange(frame_count)[:, None] >= jnp.arange(frame_count)[None, :]
    exponent = jnp.where(causal, jnp.exp(scores), 0.0)
    weight = exponent / totals[..., None]
    probability = weight.astype(jnp.bfloat16)
    prob_grad = jnp.einsum(
        "fphd,gphd->phfg", grad_four, value_four, preferred_element_type=jnp.float32
    )
    row_delta = jnp.einsum(
        "fphd,fphd->phf", grad_four, out_four, preferred_element_type=jnp.float32
    )
    score_grad = (weight * (prob_grad - row_delta[..., None])).astype(jnp.bfloat16)
    query_grad = (
        jnp.einsum("phfg,gphd->fphd", score_grad, key_four, preferred_element_type=jnp.float32)
        * score_scale
    )
    key_grad = (
        jnp.einsum("phfg,fphd->gphd", score_grad, query_four, preferred_element_type=jnp.float32)
        * score_scale
    )
    value_grad = jnp.einsum(
        "phfg,fphd->gphd", probability, grad_four, preferred_element_type=jnp.float32
    )
    pieces = [
        gradient.astype(jnp.bfloat16).reshape(frame_count, position_count, feature_count)
        for gradient in (query_grad, key_grad, value_grad)
    ]
    return jnp.concatenate(pieces, axis=-1)


def to_frames(local_rows):
    return lax.all_to_all(local_rows[None], "frame", split_axis=1, concat_axis=0, tiled=True)


def to_space(frame_rows):
    return lax.all_to_all(frame_rows, "frame", split_axis=0, concat_axis=1, tiled=True)[0]


def local(frames_in, cotangent, w_qkv_space, w_out_space, w_qkv_time, w_out_time, neighbours):
    local_in = frames_in[0]
    grad_out = cotangent[0]
    shard, feature_count = local_in.shape
    weight_rows = jnp.concatenate([w_qkv_space, w_out_space, w_qkv_time, w_out_time], axis=1)
    all_weights = lax.all_gather(weight_rows, "space", axis=0, tiled=True)
    widths = [w_qkv_space.shape[1], w_out_space.shape[1], w_qkv_time.shape[1], w_out_time.shape[1]]
    bounds = [0]
    for width in widths:
        bounds.append(bounds[-1] + width)
    full_qkv_space, full_out_space, full_qkv_time, full_out_time = (
        all_weights[:, bounds[index] : bounds[index + 1]] for index in range(4)
    )
    block_count = shard // BLOCK
    space_index = lax.axis_index("space")
    lists_here = lax.dynamic_slice_in_dim(neighbours, space_index * block_count, block_count, 0)
    allowed = block_mask(lists_here, (space_index - 1) * block_count)
    normed_space = rms_norm(local_in)
    projected = jnp.dot(normed_space, full_qkv_space, preferred_element_type=jnp.float32).astype(
        jnp.bfloat16
    )
    queries = projected[:, :feature_count]
    kv_window = padded(projected[:, feature_count:], (("space", 0),), shard)
    key_window = kv_window[:, :feature_count]
    value_window = kv_window[:, feature_count:]
    attended, totals = space_attend(queries, key_window, value_window, allowed)
    update = jnp.dot(attended, full_out_space, preferred_element_type=jnp.float32)
    stream = (local_in.astype(jnp.float32) + update).astype(jnp.bfloat16)
    normed_time = rms_norm(stream)
    projected_time = jnp.dot(normed_time, full_qkv_time, preferred_element_type=jnp.float32).astype(
        jnp.bfloat16
    )
    grad_att_time = jnp.dot(grad_out, full_out_time.T, preferred_element_type=jnp.float32).astype(
        jnp.bfloat16
    )
    time_rows = to_frames(jnp.concatenate([projected_time, grad_att_time], axis=1))
    query_time = time_rows[..., :feature_count]
    key_time = time_rows[..., feature_count : 2 * feature_count]
    value_time = time_rows[..., 2 * feature_count : 3 * feature_count]
    grad_time_rows = time_rows[..., 3 * feature_count :]
    attended_time, totals_time = time_attend(query_time, key_time, value_time)
    gradients = time_back(
        query_time, key_time, value_time, attended_time, grad_time_rows, totals_time
    )
    back_rows = to_space(jnp.concatenate([attended_time, gradients], axis=-1))
    attended_back = back_rows[:, :feature_count]
    grad_project_time = back_rows[:, feature_count:]
    update_time = jnp.dot(attended_back, full_out_time, preferred_element_type=jnp.float32)
    frames_out = (stream.astype(jnp.float32) + update_time).astype(jnp.bfloat16)
    grad_normed_time = jnp.dot(
        grad_project_time, full_qkv_time.T, preferred_element_type=jnp.float32
    )
    grad_stream = (grad_out.astype(jnp.float32) + rms_back(stream, grad_normed_time)).astype(
        jnp.bfloat16
    )
    grad_attended = jnp.dot(
        grad_stream, full_out_space.T, preferred_element_type=jnp.float32
    ).astype(jnp.bfloat16)
    grad_query, key_partial, value_partial = space_back(
        queries, key_window, value_window, allowed, totals, attended, grad_attended
    )
    kv_partial = jnp.concatenate([key_partial, value_partial], axis=1)
    kv_send = jnp.concatenate([kv_partial[:shard], kv_partial[2 * shard :]], axis=0).astype(
        jnp.bfloat16
    )
    kv_got = padded(kv_send, (("space", 0),), shard)
    grad_kv = (
        kv_partial[shard : 2 * shard]
        + kv_got[:shard].astype(jnp.float32)
        + kv_got[3 * shard :].astype(jnp.float32)
    ).astype(jnp.bfloat16)
    grad_project = jnp.concatenate([grad_query, grad_kv], axis=1)
    grad_normed = jnp.dot(grad_project, full_qkv_space.T, preferred_element_type=jnp.float32)
    grad_in = (grad_stream.astype(jnp.float32) + rms_back(local_in, grad_normed)).astype(
        jnp.bfloat16
    )
    return (frames_out[None], grad_in[None])


def solution(mesh):
    in_specs = (
        P(("dp", "frame"), "space", None),
        P(("dp", "frame"), "space", None),
        P("space", None),
        P("space", None),
        P("space", None),
        P("space", None),
        P(),
    )
    out_specs = (P(("dp", "frame"), "space", None), P(("dp", "frame"), "space", None))
    return jax.shard_map(local, mesh=mesh, in_specs=in_specs, out_specs=out_specs, check_vma=False)
```

```python
import jax
import jax.numpy as jnp
from jax import lax
from jax.sharding import PartitionSpec as P

HEADS = 12
HD = 64
BLOCK = 128


EPS = 1e-06


def padded(cells, sides, width):
    for axis, dim in sides:
        count = lax.axis_size(axis)
        ends = count - 1
        head = lax.slice_in_dim(cells, 0, width, axis=dim)
        tail = lax.slice_in_dim(cells, cells.shape[dim] - width, cells.shape[dim], axis=dim)
        cells = jnp.concatenate(
            [
                lax.ppermute(tail, axis, [(i, (i + 1) % count) for i in range(ends)]),
                cells,
                lax.ppermute(head, axis, [((i + 1) % count, i) for i in range(ends)]),
            ],
            axis=dim,
        )
    return cells


def rms_norm(row_data):
    values = row_data.astype(jnp.float32)
    factor = lax.rsqrt(jnp.mean(values * values, axis=-1, keepdims=True) + EPS)
    return (values * factor).astype(jnp.bfloat16)


def rms_back(row_data, upstream):
    values = row_data.astype(jnp.float32)
    factor = lax.rsqrt(jnp.mean(values * values, axis=-1, keepdims=True) + EPS)
    inner_mean = jnp.mean(values * upstream, axis=-1, keepdims=True)
    return factor * upstream - values * factor**3 * inner_mean


def block_mask(neighbour_rows, first_id):
    block_count = neighbour_rows.shape[0]
    candidate = first_id + jnp.arange(3 * block_count, dtype=jnp.int32)
    matches = jnp.any(neighbour_rows[:, :, None] == candidate[None, None, :], axis=1)
    return jnp.repeat(jnp.repeat(matches, BLOCK, axis=0), BLOCK, axis=1)


def space_attend(queries, key_rows, value_rows, allowed):
    score_scale = HD ** (-0.5)
    query_count = queries.shape[0]
    key_count = key_rows.shape[0]
    query_heads = queries.reshape(query_count, HEADS, HD)
    key_heads = key_rows.reshape(key_count, HEADS, HD)
    value_heads = value_rows.reshape(key_count, HEADS, HD)
    scores = (
        jnp.einsum("sgh,tgh->gst", query_heads, key_heads, preferred_element_type=jnp.float32)
        * score_scale
    )
    exponent = jnp.where(allowed[None], jnp.exp(scores), 0.0)
    totals = jnp.sum(exponent, axis=-1)
    probability = (exponent / totals[:, :, None]).astype(jnp.bfloat16)
    combined = jnp.einsum(
        "gst,tgh->sgh", probability, value_heads, preferred_element_type=jnp.float32
    )
    return combined.astype(jnp.bfloat16).reshape(query_count, HEADS * HD), totals


def space_back(queries, key_rows, value_rows, allowed, totals, attended, grad_attended):
    score_scale = HD ** (-0.5)
    query_count = queries.shape[0]
    key_count = key_rows.shape[0]
    query_heads = queries.reshape(query_count, HEADS, HD)
    key_heads = key_rows.reshape(key_count, HEADS, HD)
    value_heads = value_rows.reshape(key_count, HEADS, HD)
    out_heads = attended.reshape(query_count, HEADS, HD)
    grad_heads = grad_attended.reshape(query_count, HEADS, HD)
    scores = (
        jnp.einsum("sgh,tgh->gst", query_heads, key_heads, preferred_element_type=jnp.float32)
        * score_scale
    )
    exponent = jnp.where(allowed[None], jnp.exp(scores), 0.0)
    weight = exponent / totals[:, :, None]
    probability = weight.astype(jnp.bfloat16)
    prob_grad = jnp.einsum(
        "sgh,tgh->gst", grad_heads, value_heads, preferred_element_type=jnp.float32
    )
    row_delta = jnp.einsum(
        "sgh,sgh->gs", grad_heads, out_heads, preferred_element_type=jnp.float32
    )
    score_grad = (weight * (prob_grad - row_delta[:, :, None])).astype(jnp.bfloat16)
    query_grad = (
        jnp.einsum("gst,tgh->sgh", score_grad, key_heads, preferred_element_type=jnp.float32)
        * score_scale
    )
    key_grad = (
        jnp.einsum("gst,sgh->tgh", score_grad, query_heads, preferred_element_type=jnp.float32)
        * score_scale
    )
    value_grad = jnp.einsum(
        "gst,sgh->tgh", probability, grad_heads, preferred_element_type=jnp.float32
    )
    return (
        query_grad.astype(jnp.bfloat16).reshape(query_count, HEADS * HD),
        key_grad.reshape(key_count, HEADS * HD),
        value_grad.reshape(key_count, HEADS * HD),
    )


def time_attend(queries, key_rows, value_rows):
    frame_count, position_count, feature_count = queries.shape
    split_shape = (frame_count, position_count, HEADS, HD)
    score_scale = HD ** (-0.5)
    scores = (
        jnp.einsum(
            "fphd,gphd->phfg",
            queries.reshape(split_shape),
            key_rows.reshape(split_shape),
            preferred_element_type=jnp.float32,
        )
        * score_scale
    )
    causal = jnp.arange(frame_count)[:, None] >= jnp.arange(frame_count)[None, :]
    exponent = jnp.where(causal, jnp.exp(scores), 0.0)
    totals = jnp.sum(exponent, axis=-1)
    probability = (exponent / totals[..., None]).astype(jnp.bfloat16)
    combined = jnp.einsum(
        "phfg,gphd->fphd",
        probability,
        value_rows.reshape(split_shape),
        preferred_element_type=jnp.float32,
    )
    return (
        combined.astype(jnp.bfloat16).reshape(frame_count, position_count, feature_count),
        totals,
    )


def time_back(queries, key_rows, value_rows, attended, grad_attended, totals):
    frame_count, position_count, feature_count = queries.shape
    split_shape = (frame_count, position_count, HEADS, HD)
    score_scale = HD ** (-0.5)
    query_four = queries.reshape(split_shape)
    key_four = key_rows.reshape(split_shape)
    value_four = value_rows.reshape(split_shape)
    out_four = attended.reshape(split_shape)
    grad_four = grad_attended.reshape(split_shape)
    scores = (
        jnp.einsum("fphd,gphd->phfg", query_four, key_four, preferred_element_type=jnp.float32)
        * score_scale
    )
    causal = jnp.arange(frame_count)[:, None] >= jnp.arange(frame_count)[None, :]
    exponent = jnp.where(causal, jnp.exp(scores), 0.0)
    weight = exponent / totals[..., None]
    probability = weight.astype(jnp.bfloat16)
    prob_grad = jnp.einsum(
        "fphd,gphd->phfg", grad_four, value_four, preferred_element_type=jnp.float32
    )
    row_delta = jnp.einsum(
        "fphd,fphd->phf", grad_four, out_four, preferred_element_type=jnp.float32
    )
    score_grad = (weight * (prob_grad - row_delta[..., None])).astype(jnp.bfloat16)
    query_grad = (
        jnp.einsum("phfg,gphd->fphd", score_grad, key_four, preferred_element_type=jnp.float32)
        * score_scale
    )
    key_grad = (
        jnp.einsum("phfg,fphd->gphd", score_grad, query_four, preferred_element_type=jnp.float32)
        * score_scale
    )
    value_grad = jnp.einsum(
        "phfg,fphd->gphd", probability, grad_four, preferred_element_type=jnp.float32
    )
    pieces = [
        gradient.astype(jnp.bfloat16).reshape(frame_count, position_count, feature_count)
        for gradient in (query_grad, key_grad, value_grad)
    ]
    return jnp.concatenate(pieces, axis=-1)


def to_frames(local_rows):
    return lax.all_to_all(local_rows[None], "frame", split_axis=1, concat_axis=0, tiled=True)


def to_space(frame_rows):
    return lax.all_to_all(frame_rows, "frame", split_axis=0, concat_axis=1, tiled=True)[0]


def local(frames_in, cotangent, w_qkv_space, w_out_space, w_qkv_time, w_out_time, neighbours):
    local_in = frames_in[0]
    grad_out = cotangent[0]
    shard, feature_count = local_in.shape
    weight_rows = jnp.concatenate([w_qkv_space, w_out_space, w_qkv_time, w_out_time], axis=1)
    all_weights = lax.all_gather(weight_rows, "space", axis=0, tiled=True)
    widths = [w_qkv_space.shape[1], w_out_space.shape[1], w_qkv_time.shape[1], w_out_time.shape[1]]
    bounds = [0]
    for width in widths:
        bounds.append(bounds[-1] + width)
    full_qkv_space, full_out_space, full_qkv_time, full_out_time = (
        all_weights[:, bounds[index] : bounds[index + 1]] for index in range(4)
    )
    block_count = shard // BLOCK
    space_index = lax.axis_index("space")
    lists_here = lax.dynamic_slice_in_dim(neighbours, space_index * block_count, block_count, 0)
    allowed = block_mask(lists_here, (space_index - 1) * block_count)
    input_window = padded(local_in, (("space", 0),), shard)
    cot_rows = to_frames(grad_out)
    normed_window = rms_norm(input_window)
    normed_space = normed_window[shard : 2 * shard]
    queries = jnp.dot(
        normed_space, full_qkv_space[:, :feature_count], preferred_element_type=jnp.float32
    ).astype(jnp.bfloat16)
    kv_window = jnp.dot(
        normed_window, full_qkv_space[:, feature_count:], preferred_element_type=jnp.float32
    ).astype(jnp.bfloat16)
    key_window = kv_window[:, :feature_count]
    value_window = kv_window[:, feature_count:]
    attended, totals = space_attend(queries, key_window, value_window, allowed)
    update = jnp.dot(attended, full_out_space, preferred_element_type=jnp.float32)
    stream = (local_in.astype(jnp.float32) + update).astype(jnp.bfloat16)
    stream_rows = to_frames(stream)
    normed_time = rms_norm(stream_rows)
    projected_time = jnp.dot(normed_time, full_qkv_time, preferred_element_type=jnp.float32).astype(
        jnp.bfloat16
    )
    query_time = projected_time[..., :feature_count]
    key_time = projected_time[..., feature_count : 2 * feature_count]
    value_time = projected_time[..., 2 * feature_count :]
    attended_time, totals_time = time_attend(query_time, key_time, value_time)
    update_time = jnp.dot(attended_time, full_out_time, preferred_element_type=jnp.float32)
    frames_out_rows = (stream_rows.astype(jnp.float32) + update_time).astype(jnp.bfloat16)
    grad_att_time = jnp.dot(cot_rows, full_out_time.T, preferred_element_type=jnp.float32).astype(
        jnp.bfloat16
    )
    gradients = time_back(
        query_time, key_time, value_time, attended_time, grad_att_time, totals_time
    )
    grad_normed_time = jnp.dot(gradients, full_qkv_time.T, preferred_element_type=jnp.float32)
    grad_stream_rows = (
        cot_rows.astype(jnp.float32) + rms_back(stream_rows, grad_normed_time)
    ).astype(jnp.bfloat16)
    back_rows = to_space(jnp.concatenate([frames_out_rows, grad_stream_rows], axis=-1))
    frames_out = back_rows[:, :feature_count]
    grad_stream = back_rows[:, feature_count:]
    grad_attended = jnp.dot(
        grad_stream, full_out_space.T, preferred_element_type=jnp.float32
    ).astype(jnp.bfloat16)
    grad_query, key_partial, value_partial = space_back(
        queries, key_window, value_window, allowed, totals, attended, grad_attended
    )
    kv_partial = jnp.concatenate([key_partial, value_partial], axis=1)
    kv_send = jnp.concatenate([kv_partial[:shard], kv_partial[2 * shard :]], axis=0).astype(
        jnp.bfloat16
    )
    kv_got = padded(kv_send, (("space", 0),), shard)
    grad_kv = (
        kv_partial[shard : 2 * shard]
        + kv_got[:shard].astype(jnp.float32)
        + kv_got[3 * shard :].astype(jnp.float32)
    ).astype(jnp.bfloat16)
    grad_project = jnp.concatenate([grad_query, grad_kv], axis=1)
    grad_normed = jnp.dot(grad_project, full_qkv_space.T, preferred_element_type=jnp.float32)
    grad_in = (grad_stream.astype(jnp.float32) + rms_back(local_in, grad_normed)).astype(
        jnp.bfloat16
    )
    return (frames_out[None], grad_in[None])


def solution(mesh):
    in_specs = (
        P(("dp", "frame"), "space", None),
        P(("dp", "frame"), "space", None),
        P("space", None),
        P("space", None),
        P("space", None),
        P("space", None),
        P(),
    )
    out_specs = (P(("dp", "frame"), "space", None), P(("dp", "frame"), "space", None))
    return jax.shard_map(local, mesh=mesh, in_specs=in_specs, out_specs=out_specs, check_vma=False)
```

```python
import jax
import jax.numpy as jnp
from jax import lax
from jax.sharding import PartitionSpec as P

HEADS = 12
HD = 64
BLOCK = 128


EPS = 1e-06


def padded(cells, sides, width):
    for axis, dim in sides:
        count = lax.axis_size(axis)
        ends = count - 1
        head = lax.slice_in_dim(cells, 0, width, axis=dim)
        tail = lax.slice_in_dim(cells, cells.shape[dim] - width, cells.shape[dim], axis=dim)
        cells = jnp.concatenate(
            [
                lax.ppermute(tail, axis, [(i, (i + 1) % count) for i in range(ends)]),
                cells,
                lax.ppermute(head, axis, [((i + 1) % count, i) for i in range(ends)]),
            ],
            axis=dim,
        )
    return cells


def rms_norm(row_data):
    values = row_data.astype(jnp.float32)
    factor = lax.rsqrt(jnp.mean(values * values, axis=-1, keepdims=True) + EPS)
    return (values * factor).astype(jnp.bfloat16)


def rms_back(row_data, upstream):
    values = row_data.astype(jnp.float32)
    factor = lax.rsqrt(jnp.mean(values * values, axis=-1, keepdims=True) + EPS)
    inner_mean = jnp.mean(values * upstream, axis=-1, keepdims=True)
    return factor * upstream - values * factor**3 * inner_mean


def block_mask(neighbour_rows, first_id):
    block_count = neighbour_rows.shape[0]
    candidate = first_id + jnp.arange(3 * block_count, dtype=jnp.int32)
    matches = jnp.any(neighbour_rows[:, :, None] == candidate[None, None, :], axis=1)
    return jnp.repeat(jnp.repeat(matches, BLOCK, axis=0), BLOCK, axis=1)


def space_attend(queries, key_rows, value_rows, allowed):
    score_scale = HD ** (-0.5)
    query_count = queries.shape[0]
    key_count = key_rows.shape[0]
    query_heads = queries.reshape(query_count, HEADS, HD)
    key_heads = key_rows.reshape(key_count, HEADS, HD)
    value_heads = value_rows.reshape(key_count, HEADS, HD)
    scores = (
        jnp.einsum("sgh,tgh->gst", query_heads, key_heads, preferred_element_type=jnp.float32)
        * score_scale
    )
    exponent = jnp.where(allowed[None], jnp.exp(scores), 0.0)
    totals = jnp.sum(exponent, axis=-1)
    probability = (exponent / totals[:, :, None]).astype(jnp.bfloat16)
    combined = jnp.einsum(
        "gst,tgh->sgh", probability, value_heads, preferred_element_type=jnp.float32
    )
    return combined.astype(jnp.bfloat16).reshape(query_count, HEADS * HD), totals


def space_back(queries, key_rows, value_rows, allowed, totals, attended, grad_attended):
    score_scale = HD ** (-0.5)
    query_count = queries.shape[0]
    key_count = key_rows.shape[0]
    query_heads = queries.reshape(query_count, HEADS, HD)
    key_heads = key_rows.reshape(key_count, HEADS, HD)
    value_heads = value_rows.reshape(key_count, HEADS, HD)
    out_heads = attended.reshape(query_count, HEADS, HD)
    grad_heads = grad_attended.reshape(query_count, HEADS, HD)
    scores = (
        jnp.einsum("sgh,tgh->gst", query_heads, key_heads, preferred_element_type=jnp.float32)
        * score_scale
    )
    exponent = jnp.where(allowed[None], jnp.exp(scores), 0.0)
    weight = exponent / totals[:, :, None]
    probability = weight.astype(jnp.bfloat16)
    prob_grad = jnp.einsum(
        "sgh,tgh->gst", grad_heads, value_heads, preferred_element_type=jnp.float32
    )
    row_delta = jnp.einsum(
        "sgh,sgh->gs", grad_heads, out_heads, preferred_element_type=jnp.float32
    )
    score_grad = (weight * (prob_grad - row_delta[:, :, None])).astype(jnp.bfloat16)
    query_grad = (
        jnp.einsum("gst,tgh->sgh", score_grad, key_heads, preferred_element_type=jnp.float32)
        * score_scale
    )
    key_grad = (
        jnp.einsum("gst,sgh->tgh", score_grad, query_heads, preferred_element_type=jnp.float32)
        * score_scale
    )
    value_grad = jnp.einsum(
        "gst,sgh->tgh", probability, grad_heads, preferred_element_type=jnp.float32
    )
    return (
        query_grad.astype(jnp.bfloat16).reshape(query_count, HEADS * HD),
        key_grad.reshape(key_count, HEADS * HD),
        value_grad.reshape(key_count, HEADS * HD),
    )


def time_attend(queries, key_rows, value_rows):
    frame_count, position_count, feature_count = queries.shape
    split_shape = (frame_count, position_count, HEADS, HD)
    score_scale = HD ** (-0.5)
    scores = (
        jnp.einsum(
            "fphd,gphd->phfg",
            queries.reshape(split_shape),
            key_rows.reshape(split_shape),
            preferred_element_type=jnp.float32,
        )
        * score_scale
    )
    causal = jnp.arange(frame_count)[:, None] >= jnp.arange(frame_count)[None, :]
    exponent = jnp.where(causal, jnp.exp(scores), 0.0)
    totals = jnp.sum(exponent, axis=-1)
    probability = (exponent / totals[..., None]).astype(jnp.bfloat16)
    combined = jnp.einsum(
        "phfg,gphd->fphd",
        probability,
        value_rows.reshape(split_shape),
        preferred_element_type=jnp.float32,
    )
    return (
        combined.astype(jnp.bfloat16).reshape(frame_count, position_count, feature_count),
        totals,
    )


def time_back(queries, key_rows, value_rows, attended, grad_attended, totals):
    frame_count, position_count, feature_count = queries.shape
    split_shape = (frame_count, position_count, HEADS, HD)
    score_scale = HD ** (-0.5)
    query_four = queries.reshape(split_shape)
    key_four = key_rows.reshape(split_shape)
    value_four = value_rows.reshape(split_shape)
    out_four = attended.reshape(split_shape)
    grad_four = grad_attended.reshape(split_shape)
    scores = (
        jnp.einsum("fphd,gphd->phfg", query_four, key_four, preferred_element_type=jnp.float32)
        * score_scale
    )
    causal = jnp.arange(frame_count)[:, None] >= jnp.arange(frame_count)[None, :]
    exponent = jnp.where(causal, jnp.exp(scores), 0.0)
    weight = exponent / totals[..., None]
    probability = weight.astype(jnp.bfloat16)
    prob_grad = jnp.einsum(
        "fphd,gphd->phfg", grad_four, value_four, preferred_element_type=jnp.float32
    )
    row_delta = jnp.einsum(
        "fphd,fphd->phf", grad_four, out_four, preferred_element_type=jnp.float32
    )
    score_grad = (weight * (prob_grad - row_delta[..., None])).astype(jnp.bfloat16)
    query_grad = (
        jnp.einsum("phfg,gphd->fphd", score_grad, key_four, preferred_element_type=jnp.float32)
        * score_scale
    )
    key_grad = (
        jnp.einsum("phfg,fphd->gphd", score_grad, query_four, preferred_element_type=jnp.float32)
        * score_scale
    )
    value_grad = jnp.einsum(
        "phfg,fphd->gphd", probability, grad_four, preferred_element_type=jnp.float32
    )
    pieces = [
        gradient.astype(jnp.bfloat16).reshape(frame_count, position_count, feature_count)
        for gradient in (query_grad, key_grad, value_grad)
    ]
    return jnp.concatenate(pieces, axis=-1)


def to_frames(local_rows):
    return lax.all_to_all(local_rows[None], "frame", split_axis=1, concat_axis=0, tiled=True)


def to_space(frame_rows):
    return lax.all_to_all(frame_rows, "frame", split_axis=0, concat_axis=1, tiled=True)[0]


def local(frames_in, cotangent, w_qkv_space, w_out_space, w_qkv_time, w_out_time, neighbours):
    local_in = frames_in[0]
    grad_out = cotangent[0]
    shard, feature_count = local_in.shape
    space_rows = jnp.concatenate([w_qkv_space, w_out_space], axis=1)
    time_rows = jnp.concatenate([w_qkv_time, w_out_time], axis=1)
    mine = lax.dynamic_index_in_dim(
        jnp.stack([space_rows, time_rows]), lax.axis_index("dp"), 0, keepdims=False
    )
    all_weights = lax.all_gather(mine, ("dp", "space"), axis=0, tiled=True).reshape(
        2, -1, space_rows.shape[1]
    )
    qkv_width = w_qkv_space.shape[1]
    full_qkv_space = all_weights[0, :, :qkv_width]
    full_out_space = all_weights[0, :, qkv_width:]
    full_qkv_time = all_weights[1, :, :qkv_width]
    full_out_time = all_weights[1, :, qkv_width:]
    block_count = shard // BLOCK
    space_index = lax.axis_index("space")
    lists_here = lax.dynamic_slice_in_dim(neighbours, space_index * block_count, block_count, 0)
    allowed = block_mask(lists_here, (space_index - 1) * block_count)
    input_window = padded(local_in, (("space", 0),), shard)
    cot_rows = to_frames(grad_out)
    normed_window = rms_norm(input_window)
    normed_space = normed_window[shard : 2 * shard]
    queries = jnp.dot(
        normed_space, full_qkv_space[:, :feature_count], preferred_element_type=jnp.float32
    ).astype(jnp.bfloat16)
    kv_window = jnp.dot(
        normed_window, full_qkv_space[:, feature_count:], preferred_element_type=jnp.float32
    ).astype(jnp.bfloat16)
    key_window = kv_window[:, :feature_count]
    value_window = kv_window[:, feature_count:]
    attended, totals = space_attend(queries, key_window, value_window, allowed)
    update = jnp.dot(attended, full_out_space, preferred_element_type=jnp.float32)
    stream = (local_in.astype(jnp.float32) + update).astype(jnp.bfloat16)
    stream_rows = to_frames(stream)
    normed_time = rms_norm(stream_rows)
    projected_time = jnp.dot(normed_time, full_qkv_time, preferred_element_type=jnp.float32).astype(
        jnp.bfloat16
    )
    query_time = projected_time[..., :feature_count]
    key_time = projected_time[..., feature_count : 2 * feature_count]
    value_time = projected_time[..., 2 * feature_count :]
    attended_time, totals_time = time_attend(query_time, key_time, value_time)
    update_time = jnp.dot(attended_time, full_out_time, preferred_element_type=jnp.float32)
    frames_out_rows = (stream_rows.astype(jnp.float32) + update_time).astype(jnp.bfloat16)
    grad_att_time = jnp.dot(cot_rows, full_out_time.T, preferred_element_type=jnp.float32).astype(
        jnp.bfloat16
    )
    gradients = time_back(
        query_time, key_time, value_time, attended_time, grad_att_time, totals_time
    )
    grad_normed_time = jnp.dot(gradients, full_qkv_time.T, preferred_element_type=jnp.float32)
    grad_stream_rows = (
        cot_rows.astype(jnp.float32) + rms_back(stream_rows, grad_normed_time)
    ).astype(jnp.bfloat16)
    back_rows = to_space(jnp.concatenate([frames_out_rows, grad_stream_rows], axis=-1))
    frames_out = back_rows[:, :feature_count]
    grad_stream = back_rows[:, feature_count:]
    grad_attended = jnp.dot(
        grad_stream, full_out_space.T, preferred_element_type=jnp.float32
    ).astype(jnp.bfloat16)
    grad_query, key_partial, value_partial = space_back(
        queries, key_window, value_window, allowed, totals, attended, grad_attended
    )
    kv_partial = jnp.concatenate([key_partial, value_partial], axis=1)
    kv_send = jnp.concatenate([kv_partial[:shard], kv_partial[2 * shard :]], axis=0).astype(
        jnp.bfloat16
    )
    kv_got = padded(kv_send, (("space", 0),), shard)
    grad_kv = (
        kv_partial[shard : 2 * shard]
        + kv_got[:shard].astype(jnp.float32)
        + kv_got[3 * shard :].astype(jnp.float32)
    ).astype(jnp.bfloat16)
    grad_project = jnp.concatenate([grad_query, grad_kv], axis=1)
    grad_normed = jnp.dot(grad_project, full_qkv_space.T, preferred_element_type=jnp.float32)
    grad_in = (grad_stream.astype(jnp.float32) + rms_back(local_in, grad_normed)).astype(
        jnp.bfloat16
    )
    return (frames_out[None], grad_in[None])


def solution(mesh):
    in_specs = (
        P(("dp", "frame"), "space", None),
        P(("dp", "frame"), "space", None),
        P("space", None),
        P("space", None),
        P("space", None),
        P("space", None),
        P(),
    )
    out_specs = (P(("dp", "frame"), "space", None), P(("dp", "frame"), "space", None))
    return jax.shard_map(local, mesh=mesh, in_specs=in_specs, out_specs=out_specs, check_vma=False)
```

```python
import jax
import jax.numpy as jnp
from jax import lax
from jax.sharding import PartitionSpec as P

HEADS = 12
HD = 64
BLOCK = 128


EPS = 1e-06


def padded(cells, sides, width):
    for axis, dim in sides:
        count = lax.axis_size(axis)
        ends = count - 1
        head = lax.slice_in_dim(cells, 0, width, axis=dim)
        tail = lax.slice_in_dim(cells, cells.shape[dim] - width, cells.shape[dim], axis=dim)
        cells = jnp.concatenate(
            [
                lax.ppermute(tail, axis, [(i, (i + 1) % count) for i in range(ends)]),
                cells,
                lax.ppermute(head, axis, [((i + 1) % count, i) for i in range(ends)]),
            ],
            axis=dim,
        )
    return cells


def rms_norm(row_data):
    values = row_data.astype(jnp.float32)
    factor = lax.rsqrt(jnp.mean(values * values, axis=-1, keepdims=True) + EPS)
    return (values * factor).astype(jnp.bfloat16)


def rms_back(row_data, upstream):
    values = row_data.astype(jnp.float32)
    factor = lax.rsqrt(jnp.mean(values * values, axis=-1, keepdims=True) + EPS)
    inner_mean = jnp.mean(values * upstream, axis=-1, keepdims=True)
    return factor * upstream - values * factor**3 * inner_mean


def block_mask(neighbour_rows, first_id):
    block_count = neighbour_rows.shape[0]
    candidate = first_id + jnp.arange(3 * block_count, dtype=jnp.int32)
    matches = jnp.any(neighbour_rows[:, :, None] == candidate[None, None, :], axis=1)
    return jnp.repeat(jnp.repeat(matches, BLOCK, axis=0), BLOCK, axis=1)


def space_attend(queries, key_rows, value_rows, allowed):
    score_scale = HD ** (-0.5)
    query_count = queries.shape[0]
    key_count = key_rows.shape[0]
    query_heads = queries.reshape(query_count, HEADS, HD)
    key_heads = key_rows.reshape(key_count, HEADS, HD)
    value_heads = value_rows.reshape(key_count, HEADS, HD)
    scores = (
        jnp.einsum("sgh,tgh->gst", query_heads, key_heads, preferred_element_type=jnp.float32)
        * score_scale
    )
    exponent = jnp.where(allowed[None], jnp.exp(scores), 0.0)
    totals = jnp.sum(exponent, axis=-1)
    probability = (exponent / totals[:, :, None]).astype(jnp.bfloat16)
    combined = jnp.einsum(
        "gst,tgh->sgh", probability, value_heads, preferred_element_type=jnp.float32
    )
    return combined.astype(jnp.bfloat16).reshape(query_count, HEADS * HD), totals


def space_back(queries, key_rows, value_rows, allowed, totals, attended, grad_attended):
    score_scale = HD ** (-0.5)
    query_count = queries.shape[0]
    key_count = key_rows.shape[0]
    query_heads = queries.reshape(query_count, HEADS, HD)
    key_heads = key_rows.reshape(key_count, HEADS, HD)
    value_heads = value_rows.reshape(key_count, HEADS, HD)
    out_heads = attended.reshape(query_count, HEADS, HD)
    grad_heads = grad_attended.reshape(query_count, HEADS, HD)
    scores = (
        jnp.einsum("sgh,tgh->gst", query_heads, key_heads, preferred_element_type=jnp.float32)
        * score_scale
    )
    exponent = jnp.where(allowed[None], jnp.exp(scores), 0.0)
    weight = exponent / totals[:, :, None]
    probability = weight.astype(jnp.bfloat16)
    prob_grad = jnp.einsum(
        "sgh,tgh->gst", grad_heads, value_heads, preferred_element_type=jnp.float32
    )
    row_delta = jnp.einsum(
        "sgh,sgh->gs", grad_heads, out_heads, preferred_element_type=jnp.float32
    )
    score_grad = (weight * (prob_grad - row_delta[:, :, None])).astype(jnp.bfloat16)
    query_grad = (
        jnp.einsum("gst,tgh->sgh", score_grad, key_heads, preferred_element_type=jnp.float32)
        * score_scale
    )
    key_grad = (
        jnp.einsum("gst,sgh->tgh", score_grad, query_heads, preferred_element_type=jnp.float32)
        * score_scale
    )
    value_grad = jnp.einsum(
        "gst,sgh->tgh", probability, grad_heads, preferred_element_type=jnp.float32
    )
    return (
        query_grad.astype(jnp.bfloat16).reshape(query_count, HEADS * HD),
        key_grad.reshape(key_count, HEADS * HD),
        value_grad.reshape(key_count, HEADS * HD),
    )


def to_frames(local_rows):
    return lax.all_to_all(local_rows[None], "frame", split_axis=1, concat_axis=0, tiled=True)


def to_space(frame_rows):
    return lax.all_to_all(frame_rows, "frame", split_axis=0, concat_axis=1, tiled=True)[0]


def local(frames_in, cotangent, w_qkv_space, w_out_space, w_qkv_time, w_out_time, neighbours):
    local_in = frames_in[0]
    grad_out = cotangent[0]
    shard, feature_count = local_in.shape
    space_rows = jnp.concatenate([w_qkv_space, w_out_space], axis=1)
    time_rows = jnp.concatenate([w_qkv_time, w_out_time], axis=1)
    mine = lax.dynamic_index_in_dim(
        jnp.stack([space_rows, time_rows]), lax.axis_index("dp"), 0, keepdims=False
    )
    all_weights = lax.all_gather(mine, ("dp", "space"), axis=0, tiled=True).reshape(
        2, -1, space_rows.shape[1]
    )
    qkv_width = w_qkv_space.shape[1]
    full_qkv_space = all_weights[0, :, :qkv_width]
    full_out_space = all_weights[0, :, qkv_width:]
    full_qkv_time = all_weights[1, :, :qkv_width]
    full_out_time = all_weights[1, :, qkv_width:]
    block_count = shard // BLOCK
    space_index = lax.axis_index("space")
    lists_here = lax.dynamic_slice_in_dim(neighbours, space_index * block_count, block_count, 0)
    allowed = block_mask(lists_here, (space_index - 1) * block_count)
    input_window = padded(local_in, (("space", 0),), shard)
    cot_rows = to_frames(grad_out)
    normed_window = rms_norm(input_window)
    normed_space = normed_window[shard : 2 * shard]
    queries = jnp.dot(
        normed_space, full_qkv_space[:, :feature_count], preferred_element_type=jnp.float32
    ).astype(jnp.bfloat16)
    kv_window = jnp.dot(
        normed_window, full_qkv_space[:, feature_count:], preferred_element_type=jnp.float32
    ).astype(jnp.bfloat16)
    key_window = kv_window[:, :feature_count]
    value_window = kv_window[:, feature_count:]
    attended, totals = space_attend(queries, key_window, value_window, allowed)
    update = jnp.dot(attended, full_out_space, preferred_element_type=jnp.float32)
    stream = (local_in.astype(jnp.float32) + update).astype(jnp.bfloat16)
    stream_rows = to_frames(stream)
    normed_time = rms_norm(stream_rows)
    projected_time = jnp.dot(normed_time, full_qkv_time, preferred_element_type=jnp.float32).astype(
        jnp.bfloat16
    )
    frame_count, position_count = stream_rows.shape[:2]
    row_count = frame_count * position_count
    time_flat = projected_time.reshape(row_count, 3 * feature_count)
    query_time = time_flat[:, :feature_count]
    key_time = time_flat[:, feature_count : 2 * feature_count]
    value_time = time_flat[:, 2 * feature_count :]
    row_ids = jnp.arange(row_count, dtype=jnp.int32)
    same_position = (row_ids[:, None] % position_count) == (row_ids[None, :] % position_count)
    causal = (row_ids[None, :] // position_count) <= (row_ids[:, None] // position_count)
    allowed_time = same_position & causal
    attended_flat, totals_time = space_attend(query_time, key_time, value_time, allowed_time)
    attended_time = attended_flat.reshape(frame_count, position_count, feature_count)
    update_time = jnp.dot(attended_time, full_out_time, preferred_element_type=jnp.float32)
    frames_out_rows = (stream_rows.astype(jnp.float32) + update_time).astype(jnp.bfloat16)
    grad_att_time = jnp.dot(cot_rows, full_out_time.T, preferred_element_type=jnp.float32).astype(
        jnp.bfloat16
    )
    grad_query_time, grad_key_time, grad_value_time = space_back(
        query_time,
        key_time,
        value_time,
        allowed_time,
        totals_time,
        attended_flat,
        grad_att_time.reshape(row_count, feature_count),
    )
    gradients = jnp.concatenate(
        [grad_query_time, grad_key_time.astype(jnp.bfloat16), grad_value_time.astype(jnp.bfloat16)],
        axis=1,
    ).reshape(frame_count, position_count, 3 * feature_count)
    grad_normed_time = jnp.dot(gradients, full_qkv_time.T, preferred_element_type=jnp.float32)
    grad_stream_rows = (
        cot_rows.astype(jnp.float32) + rms_back(stream_rows, grad_normed_time)
    ).astype(jnp.bfloat16)
    back_rows = to_space(jnp.concatenate([frames_out_rows, grad_stream_rows], axis=-1))
    frames_out = back_rows[:, :feature_count]
    grad_stream = back_rows[:, feature_count:]
    grad_attended = jnp.dot(
        grad_stream, full_out_space.T, preferred_element_type=jnp.float32
    ).astype(jnp.bfloat16)
    grad_query, key_partial, value_partial = space_back(
        queries, key_window, value_window, allowed, totals, attended, grad_attended
    )
    kv_partial = jnp.concatenate([key_partial, value_partial], axis=1)
    kv_send = jnp.concatenate([kv_partial[:shard], kv_partial[2 * shard :]], axis=0).astype(
        jnp.bfloat16
    )
    kv_got = padded(kv_send, (("space", 0),), shard)
    grad_kv = (
        kv_partial[shard : 2 * shard]
        + kv_got[:shard].astype(jnp.float32)
        + kv_got[3 * shard :].astype(jnp.float32)
    ).astype(jnp.bfloat16)
    grad_project = jnp.concatenate([grad_query, grad_kv], axis=1)
    grad_normed = jnp.dot(grad_project, full_qkv_space.T, preferred_element_type=jnp.float32)
    grad_in = (grad_stream.astype(jnp.float32) + rms_back(local_in, grad_normed)).astype(
        jnp.bfloat16
    )
    return (frames_out[None], grad_in[None])


def solution(mesh):
    in_specs = (
        P(("dp", "frame"), "space", None),
        P(("dp", "frame"), "space", None),
        P("space", None),
        P("space", None),
        P("space", None),
        P("space", None),
        P(),
    )
    out_specs = (P(("dp", "frame"), "space", None), P(("dp", "frame"), "space", None))
    return jax.shard_map(local, mesh=mesh, in_specs=in_specs, out_specs=out_specs, check_vma=False)
```

```python
import jax
import jax.numpy as jnp
from jax import lax
from jax.sharding import PartitionSpec as P

HEADS = 12
HD = 64
BLOCK = 128


EPS = 1e-06


def padded(cells, sides, width):
    for axis, dim in sides:
        count = lax.axis_size(axis)
        ends = count - 1
        head = lax.slice_in_dim(cells, 0, width, axis=dim)
        tail = lax.slice_in_dim(cells, cells.shape[dim] - width, cells.shape[dim], axis=dim)
        cells = jnp.concatenate(
            [
                lax.ppermute(tail, axis, [(i, (i + 1) % count) for i in range(ends)]),
                cells,
                lax.ppermute(head, axis, [((i + 1) % count, i) for i in range(ends)]),
            ],
            axis=dim,
        )
    return cells


def rms_norm(row_data):
    values = row_data.astype(jnp.float32)
    factor = lax.rsqrt(jnp.mean(values * values, axis=-1, keepdims=True) + EPS)
    return (values * factor).astype(jnp.bfloat16)


def rms_back(row_data, upstream):
    values = row_data.astype(jnp.float32)
    factor = lax.rsqrt(jnp.mean(values * values, axis=-1, keepdims=True) + EPS)
    inner_mean = jnp.mean(values * upstream, axis=-1, keepdims=True)
    return factor * upstream - values * factor**3 * inner_mean


def block_mask(neighbour_rows, first_id):
    block_count = neighbour_rows.shape[0]
    candidate = first_id + jnp.arange(3 * block_count, dtype=jnp.int32)
    matches = jnp.any(neighbour_rows[:, :, None] == candidate[None, None, :], axis=1)
    return jnp.repeat(jnp.repeat(matches, BLOCK, axis=0), BLOCK, axis=1)


def space_attend(queries, key_rows, value_rows, allowed):
    score_scale = HD ** (-0.5)
    query_count = queries.shape[0]
    key_count = key_rows.shape[0]
    query_heads = queries.reshape(query_count, HEADS, HD)
    key_heads = key_rows.reshape(key_count, HEADS, HD)
    value_heads = value_rows.reshape(key_count, HEADS, HD)
    scores = (
        jnp.einsum("sgh,tgh->gst", query_heads, key_heads, preferred_element_type=jnp.float32)
        * score_scale
    )
    exponent = jnp.where(allowed[None], jnp.exp(scores), 0.0)
    totals = jnp.sum(exponent, axis=-1)
    probability = (exponent / totals[:, :, None]).astype(jnp.bfloat16)
    combined = jnp.einsum(
        "gst,tgh->sgh", probability, value_heads, preferred_element_type=jnp.float32
    )
    return combined.astype(jnp.bfloat16).reshape(query_count, HEADS * HD), totals


def space_back(queries, key_rows, value_rows, allowed, totals, attended, grad_attended):
    score_scale = HD ** (-0.5)
    query_count = queries.shape[0]
    key_count = key_rows.shape[0]
    query_heads = queries.reshape(query_count, HEADS, HD)
    key_heads = key_rows.reshape(key_count, HEADS, HD)
    value_heads = value_rows.reshape(key_count, HEADS, HD)
    out_heads = attended.reshape(query_count, HEADS, HD)
    grad_heads = grad_attended.reshape(query_count, HEADS, HD)
    scores = (
        jnp.einsum("sgh,tgh->gst", query_heads, key_heads, preferred_element_type=jnp.float32)
        * score_scale
    )
    exponent = jnp.where(allowed[None], jnp.exp(scores), 0.0)
    weight = exponent / totals[:, :, None]
    probability = weight.astype(jnp.bfloat16)
    prob_grad = jnp.einsum(
        "sgh,tgh->gst", grad_heads, value_heads, preferred_element_type=jnp.float32
    )
    row_delta = jnp.einsum(
        "sgh,sgh->gs", grad_heads, out_heads, preferred_element_type=jnp.float32
    )
    score_grad = (weight * (prob_grad - row_delta[:, :, None])).astype(jnp.bfloat16)
    query_grad = (
        jnp.einsum("gst,tgh->sgh", score_grad, key_heads, preferred_element_type=jnp.float32)
        * score_scale
    )
    key_grad = (
        jnp.einsum("gst,sgh->tgh", score_grad, query_heads, preferred_element_type=jnp.float32)
        * score_scale
    )
    value_grad = jnp.einsum(
        "gst,sgh->tgh", probability, grad_heads, preferred_element_type=jnp.float32
    )
    return (
        query_grad.astype(jnp.bfloat16).reshape(query_count, HEADS * HD),
        key_grad.reshape(key_count, HEADS * HD),
        value_grad.reshape(key_count, HEADS * HD),
    )


def to_frames(local_rows):
    return lax.all_to_all(local_rows[None], "frame", split_axis=1, concat_axis=0, tiled=True)


def to_space(frame_rows):
    return lax.all_to_all(frame_rows, "frame", split_axis=0, concat_axis=1, tiled=True)[0]


def local(frames_in, cotangent, w_qkv_space, w_out_space, w_qkv_time, w_out_time, neighbours):
    local_in = frames_in[0]
    grad_out = cotangent[0]
    shard, feature_count = local_in.shape
    space_rows = jnp.concatenate([w_qkv_space, w_out_space], axis=1)
    time_rows = jnp.concatenate([w_qkv_time, w_out_time], axis=1)
    mine = lax.dynamic_index_in_dim(
        jnp.stack([space_rows, time_rows]), lax.axis_index("dp"), 0, keepdims=False
    )
    all_weights = lax.all_gather(mine, ("dp", "space"), axis=0, tiled=True).reshape(
        2, -1, space_rows.shape[1]
    )
    qkv_width = w_qkv_space.shape[1]
    full_qkv_space = all_weights[0, :, :qkv_width]
    full_out_space = all_weights[0, :, qkv_width:]
    full_qkv_time = all_weights[1, :, :qkv_width]
    full_out_time = all_weights[1, :, qkv_width:]
    block_count = shard // BLOCK
    space_index = lax.axis_index("space")
    lists_here = lax.dynamic_slice_in_dim(neighbours, space_index * block_count, block_count, 0)
    allowed = block_mask(lists_here, (space_index - 1) * block_count)
    input_window = padded(local_in, (("space", 0),), shard)
    cot_rows = to_frames(grad_out)
    normed_window = rms_norm(input_window)
    normed_space = normed_window[shard : 2 * shard]
    queries = jnp.dot(
        normed_space, full_qkv_space[:, :feature_count], preferred_element_type=jnp.float32
    ).astype(jnp.bfloat16)
    kv_window = jnp.dot(
        normed_window, full_qkv_space[:, feature_count:], preferred_element_type=jnp.float32
    ).astype(jnp.bfloat16)
    key_window = kv_window[:, :feature_count]
    value_window = kv_window[:, feature_count:]
    attended, totals = space_attend(queries, key_window, value_window, allowed)
    update = jnp.dot(attended, full_out_space, preferred_element_type=jnp.float32)
    stream = (local_in.astype(jnp.float32) + update).astype(jnp.bfloat16)
    stream_rows = to_frames(stream)
    normed_time = rms_norm(stream_rows)
    projected_time = jnp.dot(normed_time, full_qkv_time, preferred_element_type=jnp.float32).astype(
        jnp.bfloat16
    )
    frame_count, position_count = stream_rows.shape[:2]
    row_count = frame_count * position_count
    time_flat = projected_time.reshape(row_count, 3 * feature_count)
    query_time = time_flat[:, :feature_count]
    key_time = time_flat[:, feature_count : 2 * feature_count]
    value_time = time_flat[:, 2 * feature_count :]
    row_ids = jnp.arange(row_count, dtype=jnp.int32)
    same_position = (row_ids[:, None] % position_count) == (row_ids[None, :] % position_count)
    causal = (row_ids[None, :] // position_count) <= (row_ids[:, None] // position_count)
    allowed_time = same_position & causal
    attended_flat, totals_time = space_attend(query_time, key_time, value_time, allowed_time)
    attended_time = attended_flat.reshape(frame_count, position_count, feature_count)
    update_time = jnp.dot(attended_time, full_out_time, preferred_element_type=jnp.float32)
    frames_out_rows = (stream_rows.astype(jnp.float32) + update_time).astype(jnp.bfloat16)
    frames_out = to_space(frames_out_rows)
    grad_att_time = jnp.dot(cot_rows, full_out_time.T, preferred_element_type=jnp.float32).astype(
        jnp.bfloat16
    )
    grad_query_time, grad_key_time, grad_value_time = space_back(
        query_time,
        key_time,
        value_time,
        allowed_time,
        totals_time,
        attended_flat,
        grad_att_time.reshape(row_count, feature_count),
    )
    gradients = jnp.concatenate(
        [grad_query_time, grad_key_time.astype(jnp.bfloat16), grad_value_time.astype(jnp.bfloat16)],
        axis=1,
    ).reshape(frame_count, position_count, 3 * feature_count)
    grad_normed_time = jnp.dot(gradients, full_qkv_time.T, preferred_element_type=jnp.float32)
    grad_stream_rows = (
        cot_rows.astype(jnp.float32) + rms_back(stream_rows, grad_normed_time)
    ).astype(jnp.bfloat16)
    grad_stream = to_space(grad_stream_rows)
    grad_attended = jnp.dot(
        grad_stream, full_out_space.T, preferred_element_type=jnp.float32
    ).astype(jnp.bfloat16)
    grad_query, key_partial, value_partial = space_back(
        queries, key_window, value_window, allowed, totals, attended, grad_attended
    )
    kv_partial = jnp.concatenate([key_partial, value_partial], axis=1)
    kv_send = jnp.concatenate([kv_partial[:shard], kv_partial[2 * shard :]], axis=0).astype(
        jnp.bfloat16
    )
    kv_got = padded(kv_send, (("space", 0),), shard)
    grad_kv = (
        kv_partial[shard : 2 * shard]
        + kv_got[:shard].astype(jnp.float32)
        + kv_got[3 * shard :].astype(jnp.float32)
    ).astype(jnp.bfloat16)
    grad_project = jnp.concatenate([grad_query, grad_kv], axis=1)
    grad_normed = jnp.dot(grad_project, full_qkv_space.T, preferred_element_type=jnp.float32)
    grad_in = (grad_stream.astype(jnp.float32) + rms_back(local_in, grad_normed)).astype(
        jnp.bfloat16
    )
    return (frames_out[None], grad_in[None])


def solution(mesh):
    in_specs = (
        P(("dp", "frame"), "space", None),
        P(("dp", "frame"), "space", None),
        P("space", None),
        P("space", None),
        P("space", None),
        P("space", None),
        P(),
    )
    out_specs = (P(("dp", "frame"), "space", None), P(("dp", "frame"), "space", None))
    return jax.shard_map(local, mesh=mesh, in_specs=in_specs, out_specs=out_specs, check_vma=False)
```

```python
import jax
import jax.numpy as jnp
from jax import lax
from jax.sharding import PartitionSpec as P

HEADS = 12
HD = 64
BLOCK = 128


EPS = 1e-06


def padded(cells, sides, width):
    for axis, dim in sides:
        count = lax.axis_size(axis)
        ends = count - 1
        head = lax.slice_in_dim(cells, 0, width, axis=dim)
        tail = lax.slice_in_dim(cells, cells.shape[dim] - width, cells.shape[dim], axis=dim)
        cells = jnp.concatenate(
            [
                lax.ppermute(tail, axis, [(i, (i + 1) % count) for i in range(ends)]),
                cells,
                lax.ppermute(head, axis, [((i + 1) % count, i) for i in range(ends)]),
            ],
            axis=dim,
        )
    return cells


def rms_norm(row_data):
    values = row_data.astype(jnp.float32)
    factor = lax.rsqrt(jnp.mean(values * values, axis=-1, keepdims=True) + EPS)
    return (values * factor).astype(jnp.bfloat16)


def rms_back(row_data, upstream):
    values = row_data.astype(jnp.float32)
    factor = lax.rsqrt(jnp.mean(values * values, axis=-1, keepdims=True) + EPS)
    inner_mean = jnp.mean(values * upstream, axis=-1, keepdims=True)
    return factor * upstream - values * factor**3 * inner_mean


def block_mask(neighbour_rows, first_id):
    block_count = neighbour_rows.shape[0]
    candidate = first_id + jnp.arange(3 * block_count, dtype=jnp.int32)
    matches = jnp.any(neighbour_rows[:, :, None] == candidate[None, None, :], axis=1)
    return jnp.repeat(jnp.repeat(matches, BLOCK, axis=0), BLOCK, axis=1)


def space_attend(queries, key_rows, value_rows, allowed):
    score_scale = HD ** (-0.5)
    query_count = queries.shape[0]
    key_count = key_rows.shape[0]
    query_heads = queries.reshape(query_count, HEADS, HD)
    key_heads = key_rows.reshape(key_count, HEADS, HD)
    value_heads = value_rows.reshape(key_count, HEADS, HD)
    scores = (
        jnp.einsum("sgh,tgh->gst", query_heads, key_heads, preferred_element_type=jnp.float32)
        * score_scale
    )
    exponent = jnp.where(allowed[None], jnp.exp(scores), 0.0)
    totals = jnp.sum(exponent, axis=-1)
    probability = (exponent / totals[:, :, None]).astype(jnp.bfloat16)
    combined = jnp.einsum(
        "gst,tgh->sgh", probability, value_heads, preferred_element_type=jnp.float32
    )
    return combined.astype(jnp.bfloat16).reshape(query_count, HEADS * HD), totals


def space_back(queries, key_rows, value_rows, allowed, totals, attended, grad_attended):
    score_scale = HD ** (-0.5)
    query_count = queries.shape[0]
    key_count = key_rows.shape[0]
    query_heads = queries.reshape(query_count, HEADS, HD)
    key_heads = key_rows.reshape(key_count, HEADS, HD)
    value_heads = value_rows.reshape(key_count, HEADS, HD)
    out_heads = attended.reshape(query_count, HEADS, HD)
    grad_heads = grad_attended.reshape(query_count, HEADS, HD)
    scores = (
        jnp.einsum("sgh,tgh->gst", query_heads, key_heads, preferred_element_type=jnp.float32)
        * score_scale
    )
    exponent = jnp.where(allowed[None], jnp.exp(scores), 0.0)
    weight = exponent / totals[:, :, None]
    probability = weight.astype(jnp.bfloat16)
    prob_grad = jnp.einsum(
        "sgh,tgh->gst", grad_heads, value_heads, preferred_element_type=jnp.float32
    )
    row_delta = jnp.einsum(
        "sgh,sgh->gs", grad_heads, out_heads, preferred_element_type=jnp.float32
    )
    score_grad = (weight * (prob_grad - row_delta[:, :, None])).astype(jnp.bfloat16)
    query_grad = (
        jnp.einsum("gst,tgh->sgh", score_grad, key_heads, preferred_element_type=jnp.float32)
        * score_scale
    )
    key_grad = (
        jnp.einsum("gst,sgh->tgh", score_grad, query_heads, preferred_element_type=jnp.float32)
        * score_scale
    )
    value_grad = jnp.einsum(
        "gst,sgh->tgh", probability, grad_heads, preferred_element_type=jnp.float32
    )
    return (
        query_grad.astype(jnp.bfloat16).reshape(query_count, HEADS * HD),
        key_grad.reshape(key_count, HEADS * HD),
        value_grad.reshape(key_count, HEADS * HD),
    )


def to_frames(local_rows):
    return lax.all_to_all(local_rows[None], "frame", split_axis=1, concat_axis=0, tiled=True)


def to_space(frame_rows):
    return lax.all_to_all(frame_rows, "frame", split_axis=0, concat_axis=1, tiled=True)[0]


def local(frames_in, cotangent, w_qkv_space, w_out_space, w_qkv_time, w_out_time, neighbours):
    local_in = frames_in[0]
    grad_out = cotangent[0]
    shard, feature_count = local_in.shape
    space_rows = jnp.concatenate([w_qkv_space, w_out_space], axis=1)
    time_rows = jnp.concatenate([w_qkv_time, w_out_time], axis=1)
    mine = lax.dynamic_index_in_dim(
        jnp.stack([space_rows, time_rows]), lax.axis_index("dp"), 0, keepdims=False
    )
    all_weights = lax.all_gather(mine, ("dp", "space"), axis=0, tiled=True).reshape(
        2, -1, space_rows.shape[1]
    )
    qkv_width = w_qkv_space.shape[1]
    full_qkv_space = all_weights[0, :, :qkv_width]
    full_out_space = all_weights[0, :, qkv_width:]
    full_qkv_time = all_weights[1, :, :qkv_width]
    full_out_time = all_weights[1, :, qkv_width:]
    block_count = shard // BLOCK
    space_index = lax.axis_index("space")
    lists_here = lax.dynamic_slice_in_dim(neighbours, space_index * block_count, block_count, 0)
    allowed = block_mask(lists_here, (space_index - 1) * block_count)
    input_window = padded(local_in, (("space", 0),), shard)
    cot_rows = to_frames(grad_out)
    normed_window = rms_norm(input_window)
    normed_space = normed_window[shard : 2 * shard]
    queries = jnp.dot(
        normed_space, full_qkv_space[:, :feature_count], preferred_element_type=jnp.float32
    ).astype(jnp.bfloat16)
    kv_window = jnp.dot(
        normed_window, full_qkv_space[:, feature_count:], preferred_element_type=jnp.float32
    ).astype(jnp.bfloat16)
    key_window = kv_window[:, :feature_count]
    value_window = kv_window[:, feature_count:]
    attended, totals = space_attend(queries, key_window, value_window, allowed)
    update = jnp.dot(attended, full_out_space, preferred_element_type=jnp.float32)
    stream = (local_in.astype(jnp.float32) + update).astype(jnp.bfloat16)
    stream_rows = to_frames(stream)
    normed_time = rms_norm(stream_rows)
    projected_time = jnp.dot(normed_time, full_qkv_time, preferred_element_type=jnp.float32).astype(
        jnp.bfloat16
    )
    frame_count, position_count = stream_rows.shape[:2]
    row_count = frame_count * position_count
    time_flat = projected_time.reshape(row_count, 3 * feature_count)
    query_time = time_flat[:, :feature_count]
    key_time = time_flat[:, feature_count : 2 * feature_count]
    value_time = time_flat[:, 2 * feature_count :]
    row_ids = jnp.arange(row_count, dtype=jnp.int32)
    same_position = (row_ids[:, None] % position_count) == (row_ids[None, :] % position_count)
    causal = (row_ids[None, :] // position_count) <= (row_ids[:, None] // position_count)
    allowed_time = same_position & causal
    attended_flat, totals_time = space_attend(query_time, key_time, value_time, allowed_time)
    attended_time = attended_flat.reshape(frame_count, position_count, feature_count)
    update_time = jnp.dot(attended_time, full_out_time, preferred_element_type=jnp.float32)
    frames_out_rows = (stream_rows.astype(jnp.float32) + update_time).astype(jnp.bfloat16)
    frames_out = to_space(frames_out_rows)
    grad_att_time = jnp.dot(cot_rows, full_out_time.T, preferred_element_type=jnp.float32).astype(
        jnp.bfloat16
    )
    grad_query_time, grad_key_time, grad_value_time = space_back(
        query_time,
        key_time,
        value_time,
        allowed_time,
        totals_time,
        attended_flat,
        grad_att_time.reshape(row_count, feature_count),
    )
    grad_normed_flat = (
        jnp.dot(grad_query_time, full_qkv_time[:, :feature_count].T, preferred_element_type=jnp.float32)
        + jnp.dot(
            grad_key_time.astype(jnp.bfloat16),
            full_qkv_time[:, feature_count : 2 * feature_count].T,
            preferred_element_type=jnp.float32,
        )
        + jnp.dot(
            grad_value_time.astype(jnp.bfloat16),
            full_qkv_time[:, 2 * feature_count :].T,
            preferred_element_type=jnp.float32,
        )
    )
    grad_normed_time = grad_normed_flat.reshape(frame_count, position_count, feature_count)
    grad_stream_rows = (
        cot_rows.astype(jnp.float32) + rms_back(stream_rows, grad_normed_time)
    ).astype(jnp.bfloat16)
    grad_stream = to_space(grad_stream_rows)
    grad_attended = jnp.dot(
        grad_stream, full_out_space.T, preferred_element_type=jnp.float32
    ).astype(jnp.bfloat16)
    grad_query, key_partial, value_partial = space_back(
        queries, key_window, value_window, allowed, totals, attended, grad_attended
    )
    kv_partial = jnp.concatenate([key_partial, value_partial], axis=1)
    kv_send = jnp.concatenate([kv_partial[:shard], kv_partial[2 * shard :]], axis=0).astype(
        jnp.bfloat16
    )
    kv_got = padded(kv_send, (("space", 0),), shard)
    grad_kv = (
        kv_partial[shard : 2 * shard]
        + kv_got[:shard].astype(jnp.float32)
        + kv_got[3 * shard :].astype(jnp.float32)
    ).astype(jnp.bfloat16)
    grad_normed = jnp.dot(
        grad_query, full_qkv_space[:, :feature_count].T, preferred_element_type=jnp.float32
    ) + jnp.dot(grad_kv, full_qkv_space[:, feature_count:].T, preferred_element_type=jnp.float32)
    grad_in = (grad_stream.astype(jnp.float32) + rms_back(local_in, grad_normed)).astype(
        jnp.bfloat16
    )
    return (frames_out[None], grad_in[None])


def solution(mesh):
    in_specs = (
        P(("dp", "frame"), "space", None),
        P(("dp", "frame"), "space", None),
        P("space", None),
        P("space", None),
        P("space", None),
        P("space", None),
        P(),
    )
    out_specs = (P(("dp", "frame"), "space", None), P(("dp", "frame"), "space", None))
    return jax.shard_map(local, mesh=mesh, in_specs=in_specs, out_specs=out_specs, check_vma=False)
```

```python
import jax
import jax.numpy as jnp
from jax import lax
from jax.sharding import PartitionSpec as P

HEADS = 12
HD = 64
BLOCK = 128


EPS = 1e-06


def padded(cells, sides, width):
    for axis, dim in sides:
        count = lax.axis_size(axis)
        ends = count - 1
        head = lax.slice_in_dim(cells, 0, width, axis=dim)
        tail = lax.slice_in_dim(cells, cells.shape[dim] - width, cells.shape[dim], axis=dim)
        cells = jnp.concatenate(
            [
                lax.ppermute(tail, axis, [(i, (i + 1) % count) for i in range(ends)]),
                cells,
                lax.ppermute(head, axis, [((i + 1) % count, i) for i in range(ends)]),
            ],
            axis=dim,
        )
    return cells


def rms_norm(row_data):
    values = row_data.astype(jnp.float32)
    factor = lax.rsqrt(jnp.mean(values * values, axis=-1, keepdims=True) + EPS)
    return (values * factor).astype(jnp.bfloat16)


def rms_back(row_data, upstream):
    values = row_data.astype(jnp.float32)
    factor = lax.rsqrt(jnp.mean(values * values, axis=-1, keepdims=True) + EPS)
    inner_mean = jnp.mean(values * upstream, axis=-1, keepdims=True)
    return factor * upstream - values * factor**3 * inner_mean


def block_mask(neighbour_rows, first_id):
    block_count = neighbour_rows.shape[0]
    candidate = first_id + jnp.arange(3 * block_count, dtype=jnp.int32)
    matches = jnp.any(neighbour_rows[:, :, None] == candidate[None, None, :], axis=1)
    return jnp.repeat(jnp.repeat(matches, BLOCK, axis=0), BLOCK, axis=1)


def space_attend(queries, key_rows, value_rows, allowed):
    score_scale = HD ** (-0.5)
    query_count = queries.shape[0]
    key_count = key_rows.shape[0]
    query_heads = queries.reshape(query_count, HEADS, HD)
    key_heads = key_rows.reshape(key_count, HEADS, HD)
    value_heads = value_rows.reshape(key_count, HEADS, HD)
    scores = (
        jnp.einsum("sgh,tgh->gst", query_heads, key_heads, preferred_element_type=jnp.float32)
        * score_scale
    )
    exponent = jnp.where(allowed[None], jnp.exp(scores), 0.0)
    totals = jnp.sum(exponent, axis=-1)
    probability = (exponent / totals[:, :, None]).astype(jnp.bfloat16)
    combined = jnp.einsum(
        "gst,tgh->sgh", probability, value_heads, preferred_element_type=jnp.float32
    )
    return combined.astype(jnp.bfloat16).reshape(query_count, HEADS * HD), totals


def space_back(queries, key_rows, value_rows, allowed, totals, attended, grad_attended):
    score_scale = HD ** (-0.5)
    query_count = queries.shape[0]
    key_count = key_rows.shape[0]
    query_heads = queries.reshape(query_count, HEADS, HD)
    key_heads = key_rows.reshape(key_count, HEADS, HD)
    value_heads = value_rows.reshape(key_count, HEADS, HD)
    out_heads = attended.reshape(query_count, HEADS, HD)
    grad_heads = grad_attended.reshape(query_count, HEADS, HD)
    scores = (
        jnp.einsum("sgh,tgh->gst", query_heads, key_heads, preferred_element_type=jnp.float32)
        * score_scale
    )
    exponent = jnp.where(allowed[None], jnp.exp(scores), 0.0)
    weight = exponent / totals[:, :, None]
    probability = weight.astype(jnp.bfloat16)
    prob_grad = jnp.einsum(
        "sgh,tgh->gst", grad_heads, value_heads, preferred_element_type=jnp.float32
    )
    row_delta = jnp.einsum(
        "sgh,sgh->gs", grad_heads, out_heads, preferred_element_type=jnp.float32
    )
    score_grad = (weight * (prob_grad - row_delta[:, :, None])).astype(jnp.bfloat16)
    query_grad = (
        jnp.einsum("gst,tgh->sgh", score_grad, key_heads, preferred_element_type=jnp.float32)
        * score_scale
    )
    key_grad = (
        jnp.einsum("gst,sgh->tgh", score_grad, query_heads, preferred_element_type=jnp.float32)
        * score_scale
    )
    value_grad = jnp.einsum(
        "gst,sgh->tgh", probability, grad_heads, preferred_element_type=jnp.float32
    )
    return (
        query_grad.astype(jnp.bfloat16).reshape(query_count, HEADS * HD),
        key_grad.reshape(key_count, HEADS * HD),
        value_grad.reshape(key_count, HEADS * HD),
    )


def to_frames(local_rows):
    return lax.all_to_all(local_rows[None], "frame", split_axis=1, concat_axis=0, tiled=True)


def to_space(frame_rows):
    return lax.all_to_all(frame_rows, "frame", split_axis=0, concat_axis=1, tiled=True)[0]


def local(frames_in, cotangent, w_qkv_space, w_out_space, w_qkv_time, w_out_time, neighbours):
    local_in = frames_in[0]
    grad_out = cotangent[0]
    shard, feature_count = local_in.shape
    space_rows = jnp.concatenate([w_qkv_space, w_out_space], axis=1)
    time_rows = jnp.concatenate([w_qkv_time, w_out_time], axis=1)
    mine = lax.dynamic_index_in_dim(
        jnp.stack([space_rows, time_rows]), lax.axis_index("dp"), 0, keepdims=False
    )
    all_weights = lax.all_gather(mine, ("dp", "space"), axis=0, tiled=True).reshape(
        2, -1, space_rows.shape[1]
    )
    qkv_width = w_qkv_space.shape[1]
    full_qkv_space = all_weights[0, :, :qkv_width]
    full_out_space = all_weights[0, :, qkv_width:]
    full_qkv_time = all_weights[1, :, :qkv_width]
    full_out_time = all_weights[1, :, qkv_width:]
    block_count = shard // BLOCK
    space_index = lax.axis_index("space")
    lists_here = lax.dynamic_slice_in_dim(neighbours, space_index * block_count, block_count, 0)
    allowed = block_mask(lists_here, (space_index - 1) * block_count)
    input_window = padded(local_in, (("space", 0),), shard)
    cot_rows = to_frames(grad_out)
    normed_window = rms_norm(input_window)
    projected_window = jnp.dot(
        normed_window, full_qkv_space, preferred_element_type=jnp.float32
    ).astype(jnp.bfloat16)
    queries = projected_window[shard : 2 * shard, :feature_count]
    key_window = projected_window[:, feature_count : 2 * feature_count]
    value_window = projected_window[:, 2 * feature_count :]
    attended, totals = space_attend(queries, key_window, value_window, allowed)
    update = jnp.dot(attended, full_out_space, preferred_element_type=jnp.float32)
    stream = (local_in.astype(jnp.float32) + update).astype(jnp.bfloat16)
    stream_rows = to_frames(stream)
    normed_time = rms_norm(stream_rows)
    projected_time = jnp.dot(normed_time, full_qkv_time, preferred_element_type=jnp.float32).astype(
        jnp.bfloat16
    )
    frame_count, position_count = stream_rows.shape[:2]
    row_count = frame_count * position_count
    time_flat = projected_time.reshape(row_count, 3 * feature_count)
    query_time = time_flat[:, :feature_count]
    key_time = time_flat[:, feature_count : 2 * feature_count]
    value_time = time_flat[:, 2 * feature_count :]
    row_ids = jnp.arange(row_count, dtype=jnp.int32)
    same_position = (row_ids[:, None] % position_count) == (row_ids[None, :] % position_count)
    causal = (row_ids[None, :] // position_count) <= (row_ids[:, None] // position_count)
    allowed_time = same_position & causal
    attended_flat, totals_time = space_attend(query_time, key_time, value_time, allowed_time)
    attended_time = attended_flat.reshape(frame_count, position_count, feature_count)
    update_time = jnp.dot(attended_time, full_out_time, preferred_element_type=jnp.float32)
    frames_out_rows = (stream_rows.astype(jnp.float32) + update_time).astype(jnp.bfloat16)
    frames_out = to_space(frames_out_rows)
    grad_att_time = jnp.dot(cot_rows, full_out_time.T, preferred_element_type=jnp.float32).astype(
        jnp.bfloat16
    )
    grad_query_time, grad_key_time, grad_value_time = space_back(
        query_time,
        key_time,
        value_time,
        allowed_time,
        totals_time,
        attended_flat,
        grad_att_time.reshape(row_count, feature_count),
    )
    gradients = jnp.concatenate(
        [grad_query_time, grad_key_time.astype(jnp.bfloat16), grad_value_time.astype(jnp.bfloat16)],
        axis=1,
    ).reshape(frame_count, position_count, 3 * feature_count)
    grad_normed_time = jnp.dot(gradients, full_qkv_time.T, preferred_element_type=jnp.float32)
    grad_stream_rows = (
        cot_rows.astype(jnp.float32) + rms_back(stream_rows, grad_normed_time)
    ).astype(jnp.bfloat16)
    grad_stream = to_space(grad_stream_rows)
    grad_attended = jnp.dot(
        grad_stream, full_out_space.T, preferred_element_type=jnp.float32
    ).astype(jnp.bfloat16)
    grad_query, key_partial, value_partial = space_back(
        queries, key_window, value_window, allowed, totals, attended, grad_attended
    )
    kv_partial = jnp.concatenate([key_partial, value_partial], axis=1)
    kv_send = jnp.concatenate([kv_partial[:shard], kv_partial[2 * shard :]], axis=0).astype(
        jnp.bfloat16
    )
    kv_got = padded(kv_send, (("space", 0),), shard)
    grad_kv = (
        kv_partial[shard : 2 * shard]
        + kv_got[:shard].astype(jnp.float32)
        + kv_got[3 * shard :].astype(jnp.float32)
    ).astype(jnp.bfloat16)
    grad_project = jnp.concatenate([grad_query, grad_kv], axis=1)
    grad_normed = jnp.dot(grad_project, full_qkv_space.T, preferred_element_type=jnp.float32)
    grad_in = (grad_stream.astype(jnp.float32) + rms_back(local_in, grad_normed)).astype(
        jnp.bfloat16
    )
    return (frames_out[None], grad_in[None])


def solution(mesh):
    in_specs = (
        P(("dp", "frame"), "space", None),
        P(("dp", "frame"), "space", None),
        P("space", None),
        P("space", None),
        P("space", None),
        P("space", None),
        P(),
    )
    out_specs = (P(("dp", "frame"), "space", None), P(("dp", "frame"), "space", None))
    return jax.shard_map(local, mesh=mesh, in_specs=in_specs, out_specs=out_specs, check_vma=False)
```

```python
import jax
import jax.numpy as jnp
from jax import lax
from jax.sharding import PartitionSpec as P

HEADS = 12
HD = 64
BLOCK = 128


EPS = 1e-06


def padded(cells, sides, width):
    for axis, dim in sides:
        count = lax.axis_size(axis)
        ends = count - 1
        head = lax.slice_in_dim(cells, 0, width, axis=dim)
        tail = lax.slice_in_dim(cells, cells.shape[dim] - width, cells.shape[dim], axis=dim)
        cells = jnp.concatenate(
            [
                lax.ppermute(tail, axis, [(i, (i + 1) % count) for i in range(ends)]),
                cells,
                lax.ppermute(head, axis, [((i + 1) % count, i) for i in range(ends)]),
            ],
            axis=dim,
        )
    return cells


def rms_norm(row_data):
    values = row_data.astype(jnp.float32)
    factor = lax.rsqrt(jnp.mean(values * values, axis=-1, keepdims=True) + EPS)
    return (values * factor).astype(jnp.bfloat16)


def rms_back(row_data, upstream):
    values = row_data.astype(jnp.float32)
    factor = lax.rsqrt(jnp.mean(values * values, axis=-1, keepdims=True) + EPS)
    inner_mean = jnp.mean(values * upstream, axis=-1, keepdims=True)
    return factor * upstream - values * factor**3 * inner_mean


def block_mask(neighbour_rows, first_id):
    block_count = neighbour_rows.shape[0]
    candidate = first_id + jnp.arange(3 * block_count, dtype=jnp.int32)
    matches = jnp.any(neighbour_rows[:, :, None] == candidate[None, None, :], axis=1)
    return jnp.repeat(jnp.repeat(matches, BLOCK, axis=0), BLOCK, axis=1)


def space_attend(queries, key_rows, value_rows, allowed):
    score_scale = HD ** (-0.5)
    query_count = queries.shape[0]
    key_count = key_rows.shape[0]
    query_heads = queries.reshape(query_count, HEADS, HD)
    key_heads = key_rows.reshape(key_count, HEADS, HD)
    value_heads = value_rows.reshape(key_count, HEADS, HD)
    scores = (
        jnp.einsum("sgh,tgh->gst", query_heads, key_heads, preferred_element_type=jnp.float32)
        * score_scale
    )
    exponent = jnp.where(allowed[None], jnp.exp(scores), 0.0)
    totals = jnp.sum(exponent, axis=-1)
    probability = (exponent / totals[:, :, None]).astype(jnp.bfloat16)
    combined = jnp.einsum(
        "gst,tgh->sgh", probability, value_heads, preferred_element_type=jnp.float32
    )
    return combined.astype(jnp.bfloat16).reshape(query_count, HEADS * HD), totals


def space_back(queries, key_rows, value_rows, allowed, totals, attended, grad_attended):
    score_scale = HD ** (-0.5)
    query_count = queries.shape[0]
    key_count = key_rows.shape[0]
    query_heads = queries.reshape(query_count, HEADS, HD)
    key_heads = key_rows.reshape(key_count, HEADS, HD)
    value_heads = value_rows.reshape(key_count, HEADS, HD)
    out_heads = attended.reshape(query_count, HEADS, HD)
    grad_heads = grad_attended.reshape(query_count, HEADS, HD)
    scores = (
        jnp.einsum("sgh,tgh->gst", query_heads, key_heads, preferred_element_type=jnp.float32)
        * score_scale
    )
    exponent = jnp.where(allowed[None], jnp.exp(scores), 0.0)
    weight = exponent / totals[:, :, None]
    probability = weight.astype(jnp.bfloat16)
    prob_grad = jnp.einsum(
        "sgh,tgh->gst", grad_heads, value_heads, preferred_element_type=jnp.float32
    )
    row_delta = jnp.einsum(
        "sgh,sgh->gs", grad_heads, out_heads, preferred_element_type=jnp.float32
    )
    score_grad = (weight * (prob_grad - row_delta[:, :, None])).astype(jnp.bfloat16)
    query_grad = (
        jnp.einsum("gst,tgh->sgh", score_grad, key_heads, preferred_element_type=jnp.float32)
        * score_scale
    )
    key_grad = (
        jnp.einsum("gst,sgh->tgh", score_grad, query_heads, preferred_element_type=jnp.float32)
        * score_scale
    )
    value_grad = jnp.einsum(
        "gst,sgh->tgh", probability, grad_heads, preferred_element_type=jnp.float32
    )
    return (
        query_grad.astype(jnp.bfloat16).reshape(query_count, HEADS * HD),
        key_grad.reshape(key_count, HEADS * HD),
        value_grad.reshape(key_count, HEADS * HD),
    )


def to_frames(local_rows):
    return lax.all_to_all(local_rows[None], "frame", split_axis=1, concat_axis=0, tiled=True)


def to_space(frame_rows):
    return lax.all_to_all(frame_rows, "frame", split_axis=0, concat_axis=1, tiled=True)[0]


def local(frames_in, cotangent, w_qkv_space, w_out_space, w_qkv_time, w_out_time, neighbours):
    local_in = frames_in[0]
    grad_out = cotangent[0]
    shard, feature_count = local_in.shape
    space_rows = jnp.concatenate([w_qkv_space, w_out_space], axis=1)
    time_rows = jnp.concatenate([w_qkv_time, w_out_time], axis=1)
    mine = lax.dynamic_index_in_dim(
        jnp.stack([space_rows, time_rows]), lax.axis_index("dp"), 0, keepdims=False
    )
    all_weights = lax.all_gather(mine, ("dp", "space"), axis=0, tiled=True).reshape(
        2, -1, space_rows.shape[1]
    )
    qkv_width = w_qkv_space.shape[1]
    full_qkv_space = all_weights[0, :, :qkv_width]
    full_out_space = all_weights[0, :, qkv_width:]
    full_qkv_time = all_weights[1, :, :qkv_width]
    full_out_time = all_weights[1, :, qkv_width:]
    block_count = shard // BLOCK
    space_index = lax.axis_index("space")
    lists_here = lax.dynamic_slice_in_dim(neighbours, space_index * block_count, block_count, 0)
    allowed = block_mask(lists_here, (space_index - 1) * block_count)
    input_window = padded(local_in, (("space", 0),), shard)
    cot_rows = to_frames(grad_out)
    normed_window = rms_norm(input_window)
    projected_window = jnp.dot(
        normed_window, full_qkv_space, preferred_element_type=jnp.float32
    ).astype(jnp.bfloat16)
    queries = projected_window[shard : 2 * shard, :feature_count]
    key_window = projected_window[:, feature_count : 2 * feature_count]
    value_window = projected_window[:, 2 * feature_count :]
    attended, totals = space_attend(queries, key_window, value_window, allowed)
    update = jnp.dot(attended, full_out_space, preferred_element_type=jnp.float32)
    stream = (local_in.astype(jnp.float32) + update).astype(jnp.bfloat16)
    stream_rows = to_frames(stream)
    normed_time = rms_norm(stream_rows)
    projected_time = jnp.dot(normed_time, full_qkv_time, preferred_element_type=jnp.float32).astype(
        jnp.bfloat16
    )
    frame_count, position_count = stream_rows.shape[:2]
    row_count = frame_count * position_count
    time_flat = projected_time.reshape(row_count, 3 * feature_count)
    query_time = time_flat[:, :feature_count]
    key_time = time_flat[:, feature_count : 2 * feature_count]
    value_time = time_flat[:, 2 * feature_count :]
    row_ids = jnp.arange(row_count, dtype=jnp.int32)
    same_position = (row_ids[:, None] % position_count) == (row_ids[None, :] % position_count)
    causal = (row_ids[None, :] // position_count) <= (row_ids[:, None] // position_count)
    allowed_time = same_position & causal
    attended_flat, totals_time = space_attend(query_time, key_time, value_time, allowed_time)
    attended_time = attended_flat.reshape(frame_count, position_count, feature_count)
    attended_back = to_space(attended_time)
    update_time = jnp.dot(attended_back, full_out_time, preferred_element_type=jnp.float32)
    frames_out = (stream.astype(jnp.float32) + update_time).astype(jnp.bfloat16)
    grad_att_time = jnp.dot(cot_rows, full_out_time.T, preferred_element_type=jnp.float32).astype(
        jnp.bfloat16
    )
    grad_query_time, grad_key_time, grad_value_time = space_back(
        query_time,
        key_time,
        value_time,
        allowed_time,
        totals_time,
        attended_flat,
        grad_att_time.reshape(row_count, feature_count),
    )
    gradients = jnp.concatenate(
        [grad_query_time, grad_key_time.astype(jnp.bfloat16), grad_value_time.astype(jnp.bfloat16)],
        axis=1,
    ).reshape(frame_count, position_count, 3 * feature_count)
    grad_normed_time = jnp.dot(gradients, full_qkv_time.T, preferred_element_type=jnp.float32)
    grad_stream_rows = (
        cot_rows.astype(jnp.float32) + rms_back(stream_rows, grad_normed_time)
    ).astype(jnp.bfloat16)
    grad_stream = to_space(grad_stream_rows)
    grad_attended = jnp.dot(
        grad_stream, full_out_space.T, preferred_element_type=jnp.float32
    ).astype(jnp.bfloat16)
    grad_query, key_partial, value_partial = space_back(
        queries, key_window, value_window, allowed, totals, attended, grad_attended
    )
    kv_partial = jnp.concatenate([key_partial, value_partial], axis=1)
    kv_send = jnp.concatenate([kv_partial[:shard], kv_partial[2 * shard :]], axis=0).astype(
        jnp.bfloat16
    )
    kv_got = padded(kv_send, (("space", 0),), shard)
    grad_kv = (
        kv_partial[shard : 2 * shard]
        + kv_got[:shard].astype(jnp.float32)
        + kv_got[3 * shard :].astype(jnp.float32)
    ).astype(jnp.bfloat16)
    grad_project = jnp.concatenate([grad_query, grad_kv], axis=1)
    grad_normed = jnp.dot(grad_project, full_qkv_space.T, preferred_element_type=jnp.float32)
    grad_in = (grad_stream.astype(jnp.float32) + rms_back(local_in, grad_normed)).astype(
        jnp.bfloat16
    )
    return (frames_out[None], grad_in[None])


def solution(mesh):
    in_specs = (
        P(("dp", "frame"), "space", None),
        P(("dp", "frame"), "space", None),
        P("space", None),
        P("space", None),
        P("space", None),
        P("space", None),
        P(),
    )
    out_specs = (P(("dp", "frame"), "space", None), P(("dp", "frame"), "space", None))
    return jax.shard_map(local, mesh=mesh, in_specs=in_specs, out_specs=out_specs, check_vma=False)
```
